32 devices in a mesh: row: 4 (over y, core), col: 8 (over z, x).
Axes of the slice: x: 2, y: 2, z: 4, core: 2. Of those that a mesh axis runs over, the one named last changes fastest.
Arguments:
- doc_embed: bfloat16 [4096, 768], P(('row', 'col')), may hold values from -6 to 6
- pair_doc: int32 [32768], P(('row', 'col')), may hold values from 0 to 127
- pair_owner: int32 [32768, 1], P(('row', 'col')), may hold values from 0 to 31; in each aligned block of 1024 rows (0 to 1023, 1024 to 2047, ...) at most 64 rows name the same one
- pair_slot: int32 [32768], P(('row', 'col')), may hold values from 0 to 95
- label_cluster: int32 [3072], P(('row', 'col')), may hold values from 0 to 255, as said below
Outputs:
- label_vectors: bfloat16 [3072, 768], P(('row', 'col'))
- centroids: bfloat16 [256, 768], replicated
- distances: float32 [3072, 256], P(('row', 'col'))
The draws below stay inside these ranges and needn't reach their ends.
Inputs may be any that keep to these rules, and one draw needn't show every extreme that they name: `pair_owner`: among the pairs of one device, at most 64 have one owner, and some owner has exactly 64. `label_cluster`: every cluster holds exactly 12 labels.
All inputs are finite; a program needn't handle non-finite values.
Results may differ from the reference program's by a relative error of at most 0.0049.
Values may be sent and summed in bfloat16 or wider, within the bound.
No kernel may reach another device: no remote copies, remote signals or barrier semaphores. Data moves between devices by JAX's collectives and lax.ppermute only.
A program may use at most 64 MiB of HBM per device.

```python
import math
import jax
import jax.numpy as jnp
import numpy as np
from jax import lax

D = 768
CLUSTERS = 256
DOC_DEV = 128
LAB_DEV = 96
PAIR_DEV = 1024
CAP = 64
DOCS = 4096
LABELS = 3072
PAIRS = 32768
N_ROW = 4
N_COL = 8


def draw_label_cluster(key, part):
    return (jax.random.permutation(key, LABELS) % CLUSTERS).astype(jnp.int32)


def place_ends(values, own_key, low, largest):
    dims = values.shape
    place = [jax.random.randint(jax.random.fold_in(own_key, axis), (), 0, dims[axis]) for axis in range(len(dims))]
    values = values.at[tuple(place)].set(low)
    longest = dims.index(max(dims))
    place[longest] = (place[longest] + 1) % dims[longest]
    return values.at[tuple(place)].set(largest)


def shard_levels(rng, extent, cuts, smallest, largest):
    loudness, own = 1.0, jax.random.fold_in(rng, 6)
    for axis_at, shards_of in cuts:
        steps = jnp.exp(jax.random.uniform(jax.random.fold_in(own, axis_at), (shards_of,), jnp.float32, smallest / len(cuts), largest / len(cuts)))
        loudness = loudness * jnp.repeat(steps, extent[axis_at] // shards_of).reshape([-1 if axis == axis_at else 1 for axis in range(len(extent))])
    return loudness


def shared_out(stream_key, own, number, rows, number_of, top, most, slope):
    ranking = jax.random.permutation(stream_key, number_of)
    heavy_load, ordinary = portions_of(number_of, rows * top, most, slope, True), portions_of(number_of, rows * top, most, slope, False)
    places = jnp.arange(number_of)

    def named(sizes, offset_by):
        used = int((sizes > 0).sum())
        fixed = max(1, used // 4)
        passed = fixed + (places - fixed + offset_by * (used - fixed)) % max(1, number_of - fixed)
        return jnp.zeros((number_of,), jnp.int32).at[ranking[jnp.where(places < fixed, places, passed)]].set(jnp.asarray(sizes, jnp.int32))

    sizes = jnp.where(number % 4 == 0, named(heavy_load, number // 4), named(ordinary, number - number // 4 - 1))
    mixed = jax.random.permutation(jax.random.fold_in(own, 3), number_of)
    source_of, sink = mixed[0:number_of // 2 * 2:2], mixed[1:number_of // 2 * 2:2]
    room = jnp.minimum(sizes[source_of] - 1, most - sizes[sink]) // 2
    room = jnp.where((source_of == ranking[0]) | (sink == ranking[0]) | (sizes[sink] == 0), 0, jnp.maximum(room, 0))
    passed = jax.random.randint(jax.random.fold_in(own, 4), (number_of // 2,), 0, 1 << 20) % (room + 1)
    sizes = sizes.at[source_of].add(-passed).at[sink].add(passed)
    labels = jnp.searchsorted(jnp.cumsum(sizes), jnp.arange(rows * top), side="right").astype(jnp.int32)
    listing = labels.reshape(top, rows).T
    listing = listing[jax.random.permutation(jax.random.fold_in(own, 1), rows)]
    offset_by = jax.random.randint(jax.random.fold_in(own, 2), (rows, 1), 0, top)
    return jnp.take_along_axis(listing, (jnp.arange(top)[None, :] + offset_by) % top, axis=1)


def portions_of(amount, total, limit, slope, full):
    portions = [(1 << 20) // math.isqrt(standing ** slope) + 1 for standing in range(1, amount + 1)]
    largest = limit if full else min(limit, max(-(-total // amount), total * portions[0] // sum(portions)))
    least = 1 if total - largest >= amount - 1 else 0
    given, rest = [largest] + [least] * (amount - 1), total - largest - least * (amount - 1)
    while rest > 0:
        free = [i for i in range(1, amount) if given[i] < largest] or [i for i in range(1, amount) if given[i] < limit]
        pool, remaining = sum([portions[i] for i in free]), rest
        for i in free:
            more = min(limit - given[i], max(1, remaining * portions[i] // pool), rest)
            given[i] = given[i] + more
            rest = rest - more
    return np.array(given)


def scatter_about(key, dims, scale, reach, cuts=(), held_as=jnp.bfloat16):
    array = scale * jax.random.normal(key, dims, jnp.float32)
    if cuts:
        array = array * shard_levels(key, dims, cuts, -0.22, 0.18)
    return jnp.clip(array, -reach, reach).astype(held_as)


def setup_inputs(seed: int = 0) -> dict:
    seeds = jax.random.split(jax.random.key(seed), 6)
    doc_embed = scatter_about(seeds[0], (DOCS, D), 1.0, 6.0, ((0, 32),))
    pair_doc = place_ends(jax.random.randint(seeds[1], (PAIRS,), 0, DOC_DEV), jax.random.fold_in(seeds[1], 1), 0, DOC_DEV - 1).astype(jnp.int32)
    pair_owner_keys = jax.random.split(jax.random.fold_in(seeds[2], 1), PAIRS // PAIR_DEV)
    pair_owner_turns = jax.random.permutation(jax.random.fold_in(seeds[2], 3), PAIRS // PAIR_DEV)
    pair_owner = jax.vmap(lambda own, number: shared_out(jax.random.fold_in(seeds[2], 2), own, number, PAIR_DEV, N_ROW * N_COL, 1, CAP, 2))(pair_owner_keys, pair_owner_turns).reshape((PAIRS, 1))
    pair_slot = place_ends(jax.random.randint(seeds[3], (PAIRS,), 0, LAB_DEV), jax.random.fold_in(seeds[3], 1), 0, LAB_DEV - 1).astype(jnp.int32)
    label_cluster = draw_label_cluster(jax.random.fold_in(seeds[5], 71), 0)
    return dict(doc_embed=doc_embed, pair_doc=pair_doc, pair_owner=pair_owner, pair_slot=pair_slot, label_cluster=label_cluster)


def rms_scale(values):
    return values * lax.rsqrt(lax.optimization_barrier(jnp.mean(values * values, axis=-1, keepdims=True)) + 1e-06)

def reference(doc_embed, pair_doc, pair_owner, pair_slot, label_cluster):
    devices = N_ROW * N_COL
    block = (jnp.arange(PAIRS, dtype=jnp.int32) // PAIR_DEV).astype(jnp.int32)
    doc_index = (block * DOC_DEV + pair_doc).astype(jnp.int32)
    label_index = (pair_owner[:, 0] * LAB_DEV + pair_slot).astype(jnp.int32)

    def add_block(total, inputs):
        doc_ids, label_ids = inputs
        return (total.at[label_ids].add(doc_embed[doc_ids].astype(jnp.float32)), None)
    label_sums, _ = lax.scan(add_block, jnp.zeros((LABELS, D), jnp.float32), (doc_index.reshape(devices, PAIR_DEV), label_index.reshape(devices, PAIR_DEV)))
    label_vectors = rms_scale(label_sums).astype(jnp.bfloat16)
    cluster_sums = jax.ops.segment_sum(label_vectors.astype(jnp.float32), label_cluster, num_segments=CLUSTERS)
    centroids = rms_scale(cluster_sums).astype(jnp.bfloat16)
    inner = jnp.dot(label_vectors, centroids.T, preferred_element_type=jnp.float32)
    distances = 1.0 - inner / float(D)
    return (label_vectors, centroids, distances)
```

```python
import jax
import jax.numpy as jnp
from jax import lax
from jax.sharding import PartitionSpec as P

CLUSTERS = 256


def rms_scale(values):
    return values * lax.rsqrt(jnp.mean(values * values, axis=-1, keepdims=True) + 1e-06)


def local(doc_embed, pair_doc, pair_owner, pair_slot, label_cluster):
    axes = ("row", "col")
    devices = lax.axis_size(axes)
    pairs = pair_doc.shape[0]
    docs, width = doc_embed.shape
    owned = label_cluster.shape[0]
    capacity = 2 * pairs // devices
    owner = pair_owner[:, 0]
    f32, bf16 = jnp.float32, jnp.bfloat16

    owner_hits = (owner[:, None] == jnp.arange(devices, dtype=jnp.int32)[None, :]).astype(bf16)
    pid = jnp.arange(pairs, dtype=jnp.int32)
    earlier = (pid[None, :] < pid[:, None]).astype(bf16)
    before = jnp.dot(earlier, owner_hits, preferred_element_type=f32)
    rank = jnp.sum(before * owner_hits.astype(f32), axis=1).astype(jnp.int32)
    position = owner * capacity + rank

    place = (jnp.arange(devices * capacity, dtype=jnp.int32)[:, None] == position[None, :]).astype(bf16)
    doc_hits = (pair_doc[:, None] == jnp.arange(docs, dtype=jnp.int32)[None, :]).astype(bf16)
    pick = jnp.dot(place, doc_hits, preferred_element_type=f32).astype(bf16)
    send_rows = jnp.dot(pick, doc_embed, preferred_element_type=f32).astype(bf16)
    slot_plus = (pair_slot + 1).astype(bf16)[:, None]
    send_slot = jnp.dot(place, slot_plus, preferred_element_type=f32)[:, 0].astype(jnp.int32) - 1

    got_rows = lax.all_to_all(
        send_rows.reshape(devices, capacity, width), axes, split_axis=0, concat_axis=0, tiled=True
    ).reshape(devices * capacity, width)
    got_slot = lax.all_to_all(
        send_slot.reshape(devices, 1, capacity), axes, split_axis=0, concat_axis=0, tiled=True
    ).reshape(devices * capacity)

    label_ids = jnp.arange(owned, dtype=jnp.int32)
    onehot = (label_ids[:, None] == got_slot[None, :]).astype(bf16)
    label_sums = jnp.dot(onehot, got_rows, preferred_element_type=f32)
    label_vectors = rms_scale(label_sums).astype(bf16)
    members = (jnp.arange(CLUSTERS, dtype=jnp.int32)[:, None] == label_cluster[None, :]).astype(bf16)
    partial_sums = jnp.dot(members, label_vectors, preferred_element_type=f32)

    if CLUSTERS % devices == 0:
        share = CLUSTERS // devices
        parts = lax.all_to_all(
            partial_sums.reshape(devices, share, width), axes, split_axis=0, concat_axis=0, tiled=True
        )
        own = rms_scale(jnp.sum(parts, axis=0)).astype(bf16)
        centroids = lax.all_to_all(
            jnp.broadcast_to(own[None], (devices, share, width)),
            axes,
            split_axis=0,
            concat_axis=0,
            tiled=True,
        ).reshape(CLUSTERS, width)
    else:
        centroids = rms_scale(lax.psum(partial_sums, axes)).astype(bf16)
    inner = lax.dot_general(
        label_vectors, centroids, (((1,), (1,)), ((), ())), preferred_element_type=f32
    )
    distances = 1.0 - inner / float(width)
    return (label_vectors, centroids, distances)


def solution(mesh):
    placed = (
        P(("row", "col"), None),
        P(("row", "col")),
        P(("row", "col"), None),
        P(("row", "col")),
        P(("row", "col")),
    )
    return jax.shard_map(
        local,
        mesh=mesh,
        in_specs=placed,
        out_specs=(P(("row", "col"), None), P(), P(("row", "col"), None)),
        check_vma=False,
    )
```

```python
import jax
import jax.numpy as jnp
from jax import lax
from jax.sharding import Mesh, PartitionSpec as P

CLUSTERS = 256


def rms_scale(values):
    return values * lax.rsqrt(jnp.mean(values * values, axis=-1, keepdims=True) + 1e-06)


def local(doc_embed, pair_doc, pair_owner, pair_slot, label_cluster):
    axes = ("y", "core", "col")
    devices = lax.axis_size(axes)
    pairs = pair_doc.shape[0]
    docs, width = doc_embed.shape
    owned = label_cluster.shape[0]
    capacity = 2 * pairs // devices
    owner = pair_owner[:, 0]
    f32, bf16 = jnp.float32, jnp.bfloat16

    owner_hits = (owner[:, None] == jnp.arange(devices, dtype=jnp.int32)[None, :]).astype(bf16)
    pid = jnp.arange(pairs, dtype=jnp.int32)
    earlier = (pid[None, :] < pid[:, None]).astype(bf16)
    before = jnp.dot(earlier, owner_hits, preferred_element_type=f32)
    rank = jnp.sum(before * owner_hits.astype(f32), axis=1).astype(jnp.int32)
    position = owner * capacity + rank

    place = (jnp.arange(devices * capacity, dtype=jnp.int32)[:, None] == position[None, :]).astype(bf16)
    tags = jnp.stack([pair_doc + 1, pair_slot + 1], axis=1).astype(bf16)
    picked = jnp.dot(place, tags, preferred_element_type=f32).astype(jnp.int32) - 1
    send_doc, send_slot = picked[:, 0], picked[:, 1]
    pick = (send_doc[:, None] == jnp.arange(docs, dtype=jnp.int32)[None, :]).astype(bf16)
    send_rows = jnp.dot(pick, doc_embed, preferred_element_type=f32).astype(bf16)

    got_rows = lax.all_to_all(
        send_rows.reshape(devices, capacity, width), axes, split_axis=0, concat_axis=0, tiled=True
    ).reshape(devices * capacity, width)
    got_slot = lax.all_to_all(
        send_slot.reshape(devices, 1, capacity), axes, split_axis=0, concat_axis=0, tiled=True
    ).reshape(devices * capacity)

    label_ids = jnp.arange(owned, dtype=jnp.int32)
    onehot = (label_ids[:, None] == got_slot[None, :]).astype(bf16)
    label_sums = jnp.dot(onehot, got_rows, preferred_element_type=f32)
    label_vectors = rms_scale(label_sums).astype(bf16)
    members = (jnp.arange(CLUSTERS, dtype=jnp.int32)[:, None] == label_cluster[None, :]).astype(bf16)
    partial_sums = jnp.dot(members, label_vectors, preferred_element_type=f32)

    if CLUSTERS % devices == 0:
        share = CLUSTERS // devices
        pair = lax.all_to_all(
            partial_sums.reshape(2, CLUSTERS // 2, width), "core", split_axis=0, concat_axis=0, tiled=True
        )
        half = jnp.sum(pair, axis=0)
        chips = ("y", "col")
        parts = lax.all_to_all(
            half.reshape(devices // 2, share, width), chips, split_axis=0, concat_axis=0, tiled=True
        )
        own = rms_scale(jnp.sum(parts, axis=0)).astype(bf16)
        half_c = lax.all_to_all(
            jnp.broadcast_to(own[None], (devices // 2, share, width)),
            chips,
            split_axis=0,
            concat_axis=0,
            tiled=True,
        ).reshape(CLUSTERS // 2, width)
        centroids = lax.all_to_all(
            jnp.broadcast_to(half_c[None], (2, CLUSTERS // 2, width)),
            "core",
            split_axis=0,
            concat_axis=0,
            tiled=True,
        ).reshape(CLUSTERS, width)
    else:
        centroids = rms_scale(lax.psum(partial_sums, axes)).astype(bf16)
    inner = lax.dot_general(
        label_vectors, centroids, (((1,), (1,)), ((), ())), preferred_element_type=f32
    )
    distances = 1.0 - inner / float(width)
    return (label_vectors, centroids, distances)


def solution(mesh):
    rows, cols = mesh.shape["row"], mesh.shape["col"]
    split = Mesh(mesh.devices.reshape(rows // 2, 2, cols), ("y", "core", "col"))
    spread = ("y", "core", "col")
    placed = (P(spread, None), P(spread), P(spread, None), P(spread), P(spread))
    return jax.shard_map(
        local,
        mesh=split,
        in_specs=placed,
        out_specs=(P(spread, None), P(), P(spread, None)),
        check_vma=False,
    )
```

```python
import jax
import jax.numpy as jnp
from jax import lax
from jax.sharding import Mesh, PartitionSpec as P

CLUSTERS = 256


def rms_scale(values):
    return values * lax.rsqrt(jnp.mean(values * values, axis=-1, keepdims=True) + 1e-06)


def local(doc_embed, pair_doc, pair_owner, pair_slot, label_cluster):
    axes = ("y", "core", "zh", "zr")
    near = ("y", "core", "zr")
    devices = lax.axis_size(axes)
    halves = lax.axis_size("zr")
    group = devices // 2
    pairs = pair_doc.shape[0]
    docs, width = doc_embed.shape
    owned = label_cluster.shape[0]
    capacity = 2 * pairs // devices
    owner = pair_owner[:, 0]
    f32, bf16 = jnp.float32, jnp.bfloat16

    owner_hits = (owner[:, None] == jnp.arange(devices, dtype=jnp.int32)[None, :]).astype(bf16)
    pid = jnp.arange(pairs, dtype=jnp.int32)
    earlier = (pid[None, :] < pid[:, None]).astype(bf16)
    before = jnp.dot(earlier, owner_hits, preferred_element_type=f32)
    rank = jnp.sum(before * owner_hits.astype(f32), axis=1).astype(jnp.int32)
    cols = 2 * halves
    o_row, o_col = owner // cols, owner % cols
    o_zh, o_zr = o_col // halves, o_col % halves
    proxy = o_row * halves + o_zr
    position = proxy * (2 * capacity) + o_zh * capacity + rank

    place = (jnp.arange(devices * capacity, dtype=jnp.int32)[:, None] == position[None, :]).astype(bf16)
    tags = jnp.stack([pair_doc + 1, pair_slot + 1], axis=1).astype(bf16)
    picked = jnp.dot(place, tags, preferred_element_type=f32).astype(jnp.int32) - 1
    send_doc, send_slot = picked[:, 0], picked[:, 1]
    pick = (send_doc[:, None] == jnp.arange(docs, dtype=jnp.int32)[None, :]).astype(bf16)
    send_rows = jnp.dot(pick, doc_embed, preferred_element_type=f32).astype(bf16)

    got_rows = lax.all_to_all(
        send_rows.reshape(group, 2 * capacity, width), near, split_axis=0, concat_axis=0, tiled=True
    ).reshape(devices * capacity, width)
    got_slot = lax.all_to_all(
        send_slot.reshape(group, 1, 2 * capacity), near, split_axis=0, concat_axis=0, tiled=True
    ).reshape(devices * capacity)

    me = lax.axis_index("zh")
    block = (jnp.arange(devices * capacity, dtype=jnp.int32) // capacity) % 2
    wanted = jnp.stack([1 - me, me])
    label_ids = jnp.arange(owned, dtype=jnp.int32)
    onehot = (
        (label_ids[None, :, None] == got_slot[None, None, :])
        & (block[None, None, :] == wanted[:, None, None])
    ).astype(bf16).reshape(2 * owned, devices * capacity)
    partial = jnp.dot(onehot, got_rows, preferred_element_type=f32)
    mirrored = lax.ppermute(partial[:owned], "zh", [(0, 1), (1, 0)])
    label_sums = partial[owned:] + mirrored
    label_vectors = rms_scale(label_sums).astype(bf16)
    members = (jnp.arange(CLUSTERS, dtype=jnp.int32)[:, None] == label_cluster[None, :]).astype(bf16)
    partial_sums = jnp.dot(members, label_vectors, preferred_element_type=f32)

    if CLUSTERS % devices == 0:
        share = CLUSTERS // devices
        pair = lax.all_to_all(
            partial_sums.reshape(2, CLUSTERS // 2, width), "core", split_axis=0, concat_axis=0, tiled=True
        )
        half = jnp.sum(pair, axis=0)
        chips = ("y", "zh", "zr")
        parts = lax.all_to_all(
            half.reshape(devices // 2, share, width), chips, split_axis=0, concat_axis=0, tiled=True
        )
        own = rms_scale(jnp.sum(parts, axis=0)).astype(bf16)
        half_c = lax.all_to_all(
            jnp.broadcast_to(own[None], (devices // 2, share, width)),
            chips,
            split_axis=0,
            concat_axis=0,
            tiled=True,
        ).reshape(CLUSTERS // 2, width)
        centroids = lax.all_to_all(
            jnp.broadcast_to(half_c[None], (2, CLUSTERS // 2, width)),
            "core",
            split_axis=0,
            concat_axis=0,
            tiled=True,
        ).reshape(CLUSTERS, width)
    else:
        centroids = rms_scale(lax.psum(partial_sums, axes)).astype(bf16)
    inner = lax.dot_general(
        label_vectors, centroids, (((1,), (1,)), ((), ())), preferred_element_type=f32
    )
    distances = 1.0 - inner / float(width)
    return (label_vectors, centroids, distances)


def solution(mesh):
    rows, cols = mesh.shape["row"], mesh.shape["col"]
    split = Mesh(mesh.devices.reshape(rows // 2, 2, 2, cols // 2), ("y", "core", "zh", "zr"))
    spread = ("y", "core", "zh", "zr")
    placed = (P(spread, None), P(spread), P(spread, None), P(spread), P(spread))
    return jax.shard_map(
        local,
        mesh=split,
        in_specs=placed,
        out_specs=(P(spread, None), P(), P(spread, None)),
        check_vma=False,
    )
```

```python
import jax
import jax.numpy as jnp
from jax import lax
from jax.sharding import Mesh, PartitionSpec as P

CLUSTERS = 256


def rms_scale(values):
    return values * lax.rsqrt(jnp.mean(values * values, axis=-1, keepdims=True) + 1e-06)


def local(doc_embed, pair_doc, pair_owner, pair_slot, label_cluster):
    axes = ("y", "core", "zh", "zr")
    near = ("y", "core", "zr")
    devices = lax.axis_size(axes)
    halves = lax.axis_size("zr")
    group = devices // 2
    pairs = pair_doc.shape[0]
    docs, width = doc_embed.shape
    owned = label_cluster.shape[0]
    capacity = 2 * pairs // devices
    owner = pair_owner[:, 0]
    f32, bf16 = jnp.float32, jnp.bfloat16

    owner_hits = (owner[:, None] == jnp.arange(devices, dtype=jnp.int32)[None, :]).astype(bf16)
    pid = jnp.arange(pairs, dtype=jnp.int32)
    earlier = (pid[None, :] < pid[:, None]).astype(bf16)
    before = jnp.dot(earlier, owner_hits, preferred_element_type=f32)
    rank = jnp.sum(before * owner_hits.astype(f32), axis=1).astype(jnp.int32)
    cols = 2 * halves
    o_row, o_col = owner // cols, owner % cols
    o_zh, o_zr = o_col // halves, o_col % halves
    proxy = o_row * halves + o_zr
    position = proxy * (2 * capacity) + o_zh * capacity + rank

    place = (jnp.arange(devices * capacity, dtype=jnp.int32)[:, None] == position[None, :]).astype(bf16)
    tags = jnp.stack([pair_doc + 1, pair_slot + 1], axis=1).astype(bf16)
    picked = jnp.dot(place, tags, preferred_element_type=f32).astype(jnp.int32) - 1
    send_doc, send_slot = picked[:, 0], picked[:, 1]
    pick = (send_doc[:, None] == jnp.arange(docs, dtype=jnp.int32)[None, :]).astype(bf16)
    send_rows = jnp.dot(pick, doc_embed, preferred_element_type=f32).astype(bf16)

    got_rows = lax.all_to_all(
        send_rows.reshape(group, 2 * capacity, width), near, split_axis=0, concat_axis=0, tiled=True
    ).reshape(devices * capacity, width)
    got_slot = lax.all_to_all(
        send_slot.reshape(group, 1, 2 * capacity), near, split_axis=0, concat_axis=0, tiled=True
    ).reshape(devices * capacity)

    me = lax.axis_index("zh")
    block = (jnp.arange(devices * capacity, dtype=jnp.int32) // capacity) % 2
    wanted = jnp.stack([1 - me, me])
    label_ids = jnp.arange(owned, dtype=jnp.int32)
    onehot = (
        (label_ids[None, :, None] == got_slot[None, None, :])
        & (block[None, None, :] == wanted[:, None, None])
    ).astype(bf16).reshape(2 * owned, devices * capacity)
    partial = jnp.dot(onehot, got_rows, preferred_element_type=f32)
    mirrored = lax.ppermute(partial[:owned], "zh", [(0, 1), (1, 0)])
    label_sums = partial[owned:] + mirrored
    label_vectors = rms_scale(label_sums).astype(bf16)
    members = (jnp.arange(CLUSTERS, dtype=jnp.int32)[:, None] == label_cluster[None, :]).astype(bf16)
    partial_sums = jnp.dot(members, label_vectors, preferred_element_type=f32)

    if CLUSTERS % group == 0:
        share = CLUSTERS // group
        parts = lax.all_to_all(
            partial_sums.reshape(group, share, width), near, split_axis=0, concat_axis=0, tiled=True
        )
        half_sums = jnp.sum(parts, axis=0)
        sums = half_sums + lax.ppermute(half_sums, "zh", [(0, 1), (1, 0)])
        own = rms_scale(sums).astype(bf16)
        centroids = lax.all_to_all(
            jnp.broadcast_to(own[None], (group, share, width)),
            near,
            split_axis=0,
            concat_axis=0,
            tiled=True,
        ).reshape(CLUSTERS, width)
    else:
        centroids = rms_scale(lax.psum(partial_sums, axes)).astype(bf16)
    inner = lax.dot_general(
        label_vectors, centroids, (((1,), (1,)), ((), ())), preferred_element_type=f32
    )
    distances = 1.0 - inner / float(width)
    return (label_vectors, centroids, distances)


def solution(mesh):
    rows, cols = mesh.shape["row"], mesh.shape["col"]
    split = Mesh(mesh.devices.reshape(rows // 2, 2, 2, cols // 2), ("y", "core", "zh", "zr"))
    spread = ("y", "core", "zh", "zr")
    placed = (P(spread, None), P(spread), P(spread, None), P(spread), P(spread))
    return jax.shard_map(
        local,
        mesh=split,
        in_specs=placed,
        out_specs=(P(spread, None), P(), P(spread, None)),
        check_vma=False,
    )
```

```python
import jax
import jax.numpy as jnp
from jax import lax
from jax.sharding import Mesh, PartitionSpec as P

CLUSTERS = 256


def rms_scale(values):
    return values * lax.rsqrt(jnp.mean(values * values, axis=-1, keepdims=True) + 1e-06)


def local(doc_embed, pair_doc, pair_owner, pair_slot, label_cluster):
    axes = ("y", "core", "zh", "zr")
    near = ("y", "core", "zr")
    devices = lax.axis_size(axes)
    halves = lax.axis_size("zr")
    group = devices // 2
    pairs = pair_doc.shape[0]
    docs, width = doc_embed.shape
    owned = label_cluster.shape[0]
    capacity = 2 * pairs // devices
    owner = pair_owner[:, 0]
    f32, bf16 = jnp.float32, jnp.bfloat16

    owner_hits = (owner[:, None] == jnp.arange(devices, dtype=jnp.int32)[None, :]).astype(bf16)
    pid = jnp.arange(pairs, dtype=jnp.int32)
    earlier = (pid[None, :] < pid[:, None]).astype(bf16)
    before = jnp.dot(earlier, owner_hits, preferred_element_type=f32)
    rank = jnp.sum(before * owner_hits.astype(f32), axis=1).astype(jnp.int32)
    cols = 2 * halves
    o_row, o_col = owner // cols, owner % cols
    o_zh, o_zr = o_col // halves, o_col % halves
    proxy = o_row * halves + o_zr
    position = proxy * (2 * capacity) + o_zh * capacity + rank

    place = (jnp.arange(devices * capacity, dtype=jnp.int32)[:, None] == position[None, :]).astype(bf16)
    tags = jnp.stack([pair_doc + 1, pair_slot + 1], axis=1).astype(bf16)
    picked = jnp.dot(place, tags, preferred_element_type=f32).astype(jnp.int32)
    send_doc, slot_plus = picked[:, 0] - 1, picked[:, 1]

    span, extra = 2 * capacity, 16
    doc_part = (send_doc[:, None] == jnp.arange(docs, dtype=jnp.int32)[None, :]).astype(bf16)
    doc_part = jnp.concatenate(
        [doc_part.reshape(group, span, docs), jnp.zeros((group, extra, docs), bf16)], axis=1
    )
    slot_row = slot_plus.astype(bf16).reshape(group, 1, span)
    slot_part = jnp.concatenate(
        [jnp.zeros((group, span, span), bf16), slot_row, jnp.zeros((group, extra - 1, span), bf16)],
        axis=1,
    )
    chooser = jnp.concatenate([doc_part, slot_part], axis=2).reshape(group * (span + extra), docs + span)
    table = jnp.concatenate([doc_embed, jnp.eye(span, width, dtype=bf16)], axis=0)
    send = jnp.dot(chooser, table, preferred_element_type=f32).astype(bf16)

    got = lax.all_to_all(
        send.reshape(group, span + extra, width), near, split_axis=0, concat_axis=0, tiled=True
    )
    got_slot = got[:, span, :span].astype(jnp.int32).reshape(devices * capacity) - 1
    got_rows = got.reshape(group * (span + extra), width)

    me = lax.axis_index("zh")
    block = (jnp.arange(devices * capacity, dtype=jnp.int32) // capacity) % 2
    wanted = jnp.stack([1 - me, me])
    label_ids = jnp.arange(owned, dtype=jnp.int32)
    onehot = (
        (label_ids[None, :, None] == got_slot[None, None, :])
        & (block[None, None, :] == wanted[:, None, None])
    ).astype(bf16).reshape(2 * owned, group, span)
    onehot = jnp.concatenate([onehot, jnp.zeros((2 * owned, group, extra), bf16)], axis=2)
    onehot = onehot.reshape(2 * owned, group * (span + extra))
    partial = jnp.dot(onehot, got_rows, preferred_element_type=f32)
    mirrored = lax.ppermute(partial[:owned], "zh", [(0, 1), (1, 0)])
    label_sums = partial[owned:] + mirrored
    label_vectors = rms_scale(label_sums).astype(bf16)
    members = (jnp.arange(CLUSTERS, dtype=jnp.int32)[:, None] == label_cluster[None, :]).astype(bf16)
    partial_sums = jnp.dot(members, label_vectors, preferred_element_type=f32)

    if CLUSTERS % group == 0:
        share = CLUSTERS // group
        parts = lax.all_to_all(
            partial_sums.reshape(group, share, width), near, split_axis=0, concat_axis=0, tiled=True
        )
        half_sums = jnp.sum(parts, axis=0)
        sums = half_sums + lax.ppermute(half_sums, "zh", [(0, 1), (1, 0)])
        own = rms_scale(sums).astype(bf16)
        centroids = lax.all_to_all(
            jnp.broadcast_to(own[None], (group, share, width)),
            near,
            split_axis=0,
            concat_axis=0,
            tiled=True,
        ).reshape(CLUSTERS, width)
    else:
        centroids = rms_scale(lax.psum(partial_sums, axes)).astype(bf16)
    inner = lax.dot_general(
        label_vectors, centroids, (((1,), (1,)), ((), ())), preferred_element_type=f32
    )
    distances = 1.0 - inner / float(width)
    return (label_vectors, centroids, distances)


def solution(mesh):
    rows, cols = mesh.shape["row"], mesh.shape["col"]
    split = Mesh(mesh.devices.reshape(rows // 2, 2, 2, cols // 2), ("y", "core", "zh", "zr"))
    spread = ("y", "core", "zh", "zr")
    placed = (P(spread, None), P(spread), P(spread, None), P(spread), P(spread))
    return jax.shard_map(
        local,
        mesh=split,
        in_specs=placed,
        out_specs=(P(spread, None), P(), P(spread, None)),
        check_vma=False,
    )
```

```python
import jax
import jax.numpy as jnp
from jax import lax
from jax.sharding import Mesh, PartitionSpec as P

CLUSTERS = 256


def rms_scale(values):
    return values * lax.rsqrt(jnp.mean(values * values, axis=-1, keepdims=True) + 1e-06)


def local(doc_embed, pair_doc, pair_owner, pair_slot, label_cluster):
    axes = ("y", "core", "zh", "zr")
    near = ("y", "core", "zr")
    devices = lax.axis_size(axes)
    halves = lax.axis_size("zr")
    group = devices // 2
    pairs = pair_doc.shape[0]
    docs, width = doc_embed.shape
    owned = label_cluster.shape[0]
    capacity = 2 * pairs // devices
    owner = pair_owner[:, 0]
    f32, bf16 = jnp.float32, jnp.bfloat16

    owner_hits = (owner[:, None] == jnp.arange(devices, dtype=jnp.int32)[None, :]).astype(bf16)
    pid = jnp.arange(pairs, dtype=jnp.int32)
    earlier = (pid[None, :] < pid[:, None]).astype(bf16)
    before = jnp.dot(earlier, owner_hits, preferred_element_type=f32)
    rank = jnp.sum(before * owner_hits.astype(f32), axis=1).astype(jnp.int32)
    cols = 2 * halves
    o_row, o_col = owner // cols, owner % cols
    o_zh, o_zr = o_col // halves, o_col % halves
    proxy = o_row * halves + o_zr
    position = proxy * (2 * capacity) + o_zh * capacity + rank

    place = (jnp.arange(devices * capacity, dtype=jnp.int32)[:, None] == position[None, :]).astype(bf16)
    tags = jnp.stack([pair_doc + 1, pair_slot + 1], axis=1).astype(bf16)
    picked = jnp.dot(place, tags, preferred_element_type=f32).astype(jnp.int32)
    send_doc, slot_plus = picked[:, 0] - 1, picked[:, 1]

    span, extra = 2 * capacity, 16
    doc_part = (send_doc[:, None] == jnp.arange(docs, dtype=jnp.int32)[None, :]).astype(bf16)
    doc_part = jnp.concatenate(
        [doc_part.reshape(group, span, docs), jnp.zeros((group, extra, docs), bf16)], axis=1
    )
    slot_row = slot_plus.astype(bf16).reshape(group, 1, span)
    slot_part = jnp.concatenate(
        [jnp.zeros((group, span, span), bf16), slot_row, jnp.zeros((group, extra - 1, span), bf16)],
        axis=1,
    )
    chooser = jnp.concatenate([doc_part, slot_part], axis=2).reshape(group * (span + extra), docs + span)
    table = jnp.concatenate([doc_embed, jnp.eye(span, width, dtype=bf16)], axis=0)
    send = jnp.dot(chooser, table, preferred_element_type=f32).astype(bf16)

    got = lax.all_to_all(
        send.reshape(group, span + extra, width), near, split_axis=0, concat_axis=0, tiled=True
    )
    got_slot = jnp.concatenate(
        [got[:, span, :span].astype(jnp.int32) - 1, jnp.full((group, extra), -1, jnp.int32)], axis=1
    ).reshape(group * (span + extra))
    got_rows = got.reshape(group * (span + extra), width)

    me = lax.axis_index("zh")
    block = (jnp.arange(group * (span + extra), dtype=jnp.int32) % (span + extra)) // capacity
    row_label = jnp.arange(2 * owned, dtype=jnp.int32) % owned
    row_block = jnp.where(jnp.arange(2 * owned, dtype=jnp.int32) < owned, 1 - me, me)
    onehot = (
        (row_label[:, None] == got_slot[None, :]) & (row_block[:, None] == block[None, :])
    ).astype(bf16)
    partial = jnp.dot(onehot, got_rows, preferred_element_type=f32)
    mirrored = lax.ppermute(partial[:owned], "zh", [(0, 1), (1, 0)])
    label_sums = partial[owned:] + mirrored
    label_vectors = rms_scale(label_sums).astype(bf16)
    members = (jnp.arange(CLUSTERS, dtype=jnp.int32)[:, None] == label_cluster[None, :]).astype(bf16)
    partial_sums = jnp.dot(members, label_vectors, preferred_element_type=f32)

    if CLUSTERS % group == 0:
        share = CLUSTERS // group
        parts = lax.all_to_all(
            partial_sums.reshape(group, share, width), near, split_axis=0, concat_axis=0, tiled=True
        )
        half_sums = jnp.sum(parts, axis=0)
        sums = half_sums + lax.ppermute(half_sums, "zh", [(0, 1), (1, 0)])
        own = rms_scale(sums).astype(bf16)
        centroids = lax.all_to_all(
            jnp.broadcast_to(own[None], (group, share, width)),
            near,
            split_axis=0,
            concat_axis=0,
            tiled=True,
        ).reshape(CLUSTERS, width)
    else:
        centroids = rms_scale(lax.psum(partial_sums, axes)).astype(bf16)
    inner = lax.dot_general(
        label_vectors, centroids, (((1,), (1,)), ((), ())), preferred_element_type=f32
    )
    distances = 1.0 - inner / float(width)
    return (label_vectors, centroids, distances)


def solution(mesh):
    rows, cols = mesh.shape["row"], mesh.shape["col"]
    split = Mesh(mesh.devices.reshape(rows // 2, 2, 2, cols // 2), ("y", "core", "zh", "zr"))
    spread = ("y", "core", "zh", "zr")
    placed = (P(spread, None), P(spread), P(spread, None), P(spread), P(spread))
    return jax.shard_map(
        local,
        mesh=split,
        in_specs=placed,
        out_specs=(P(spread, None), P(), P(spread, None)),
        check_vma=False,
    )
```

```python
import jax
import jax.numpy as jnp
from jax import lax
from jax.sharding import Mesh, PartitionSpec as P

CLUSTERS = 256


def rms_scale(values):
    return values * lax.rsqrt(jnp.mean(values * values, axis=-1, keepdims=True) + 1e-06)


def local(doc_embed, pair_doc, pair_owner, pair_slot, label_cluster):
    axes = ("y", "core", "zh", "zr")
    near = ("y", "core", "zr")
    devices = lax.axis_size(axes)
    halves = lax.axis_size("zr")
    group = devices // 2
    pairs = pair_doc.shape[0]
    docs, width = doc_embed.shape
    owned = label_cluster.shape[0]
    capacity = 2 * pairs // devices
    owner = pair_owner[:, 0]
    f32, bf16 = jnp.float32, jnp.bfloat16

    owner_hits = (owner[:, None] == jnp.arange(devices, dtype=jnp.int32)[None, :]).astype(bf16)
    pid = jnp.arange(pairs, dtype=jnp.int32)
    earlier = (pid[None, :] < pid[:, None]).astype(bf16)
    before = jnp.dot(earlier, owner_hits, preferred_element_type=f32)
    rank = jnp.sum(before * owner_hits.astype(f32), axis=1).astype(jnp.int32)
    cols = 2 * halves
    o_row, o_col = owner // cols, owner % cols
    o_zh, o_zr = o_col // halves, o_col % halves
    proxy = o_row * halves + o_zr
    me = lax.axis_index("zh")
    later = (o_zh == me).astype(jnp.int32)
    position = later * (group * capacity) + proxy * capacity + rank

    place = (jnp.arange(devices * capacity, dtype=jnp.int32)[:, None] == position[None, :]).astype(bf16)
    tags = (jnp.stack([pair_doc, pair_slot], axis=1) + 1).astype(bf16)
    picked = jnp.dot(place, tags, preferred_element_type=f32).astype(jnp.int32)
    send_doc, slot_plus = picked[:, 0] - 1, picked[:, 1]
    first_doc, second_doc = send_doc[: group * capacity], send_doc[group * capacity :]

    extra = 16
    doc_part = (first_doc[:, None] == jnp.arange(docs, dtype=jnp.int32)[None, :]).astype(bf16)
    doc_part = jnp.concatenate(
        [doc_part.reshape(group, capacity, docs), jnp.zeros((group, extra, docs), bf16)], axis=1
    )
    slot_row = slot_plus.astype(bf16).reshape(2, group, capacity).transpose(1, 0, 2)
    slot_row = slot_row.reshape(group, 1, 2 * capacity)
    slot_part = jnp.concatenate(
        [
            jnp.zeros((group, capacity, 2 * capacity), bf16),
            slot_row,
            jnp.zeros((group, extra - 1, 2 * capacity), bf16),
        ],
        axis=1,
    )
    chooser = jnp.concatenate([doc_part, slot_part], axis=2)
    chooser = chooser.reshape(group * (capacity + extra), docs + 2 * capacity)
    table = jnp.concatenate([doc_embed, jnp.eye(2 * capacity, width, dtype=bf16)], axis=0)
    send_first = jnp.dot(chooser, table, preferred_element_type=f32).astype(bf16)
    pick = (second_doc[:, None] == jnp.arange(docs, dtype=jnp.int32)[None, :]).astype(bf16)
    send_second = jnp.dot(pick, doc_embed, preferred_element_type=f32).astype(bf16)

    got_first = lax.all_to_all(
        send_first.reshape(group, capacity + extra, width), near, split_axis=0, concat_axis=0, tiled=True
    )
    got_second = lax.all_to_all(
        send_second.reshape(group, capacity, width), near, split_axis=0, concat_axis=0, tiled=True
    )
    slots = got_first[:, capacity, : 2 * capacity].astype(jnp.int32) - 1
    first_slot = jnp.concatenate(
        [slots[:, :capacity], jnp.full((group, extra), -1, jnp.int32)], axis=1
    ).reshape(group * (capacity + extra))
    second_slot = slots[:, capacity:].reshape(group * capacity)

    label_ids = jnp.arange(owned, dtype=jnp.int32)
    first_hot = (label_ids[:, None] == first_slot[None, :]).astype(bf16)
    mirror_part = jnp.dot(
        first_hot, got_first.reshape(group * (capacity + extra), width), preferred_element_type=f32
    )
    mirrored = lax.ppermute(mirror_part, "zh", [(0, 1), (1, 0)])
    second_hot = (label_ids[:, None] == second_slot[None, :]).astype(bf16)
    own_part = jnp.dot(
        second_hot, got_second.reshape(group * capacity, width), preferred_element_type=f32
    )
    label_sums = own_part + mirrored
    label_vectors = rms_scale(label_sums).astype(bf16)
    members = (jnp.arange(CLUSTERS, dtype=jnp.int32)[:, None] == label_cluster[None, :]).astype(bf16)
    partial_sums = jnp.dot(members, label_vectors, preferred_element_type=f32)

    if CLUSTERS % group == 0:
        share = CLUSTERS // group
        parts = lax.all_to_all(
            partial_sums.reshape(group, share, width), near, split_axis=0, concat_axis=0, tiled=True
        )
        half_sums = jnp.sum(parts, axis=0)
        sums = half_sums + lax.ppermute(half_sums, "zh", [(0, 1), (1, 0)])
        own = rms_scale(sums).astype(bf16)
        centroids = lax.all_to_all(
            jnp.broadcast_to(own[None], (group, share, width)),
            near,
            split_axis=0,
            concat_axis=0,
            tiled=True,
        ).reshape(CLUSTERS, width)
    else:
        centroids = rms_scale(lax.psum(partial_sums, axes)).astype(bf16)
    inner = lax.dot_general(
        label_vectors, centroids, (((1,), (1,)), ((), ())), preferred_element_type=f32
    )
    distances = 1.0 - inner / float(width)
    return (label_vectors, centroids, distances)


def solution(mesh):
    rows, cols = mesh.shape["row"], mesh.shape["col"]
    split = Mesh(mesh.devices.reshape(rows // 2, 2, 2, cols // 2), ("y", "core", "zh", "zr"))
    spread = ("y", "core", "zh", "zr")
    placed = (P(spread, None), P(spread), P(spread, None), P(spread), P(spread))
    return jax.shard_map(
        local,
        mesh=split,
        in_specs=placed,
        out_specs=(P(spread, None), P(), P(spread, None)),
        check_vma=False,
    )
```

```python
import jax
import jax.numpy as jnp
from jax import lax
from jax.sharding import Mesh, PartitionSpec as P

CLUSTERS = 256


def rms_scale(values):
    return values * lax.rsqrt(jnp.mean(values * values, axis=-1, keepdims=True) + 1e-06)


def local(doc_embed, pair_doc, pair_owner, pair_slot, label_cluster):
    axes = ("y", "core", "zh", "zr")
    near = ("y", "core", "zr")
    devices = lax.axis_size(axes)
    halves = lax.axis_size("zr")
    group = devices // 2
    pairs = pair_doc.shape[0]
    docs, width = doc_embed.shape
    owned = label_cluster.shape[0]
    capacity = 2 * pairs // devices
    owner = pair_owner[:, 0]
    f32, bf16 = jnp.float32, jnp.bfloat16

    owner_hits = (owner[:, None] == jnp.arange(devices, dtype=jnp.int32)[None, :]).astype(bf16)
    pid = jnp.arange(pairs, dtype=jnp.int32)
    earlier = (pid[None, :] < pid[:, None]).astype(bf16)
    before = jnp.dot(earlier, owner_hits, preferred_element_type=f32)
    rank = jnp.sum(before * owner_hits.astype(f32), axis=1).astype(jnp.int32)
    cols = 2 * halves
    o_row, o_col = owner // cols, owner % cols
    o_zh, o_zr = o_col // halves, o_col % halves
    proxy = o_row * halves + o_zr
    me = lax.axis_index("zh")
    later = (o_zh == me).astype(jnp.int32)
    position = later * (group * capacity) + proxy * capacity + rank

    place = (jnp.arange(devices * capacity, dtype=jnp.int32)[:, None] == position[None, :]).astype(bf16)
    tags = (jnp.stack([pair_doc, pair_slot], axis=1) + 1).astype(bf16)
    picked = jnp.dot(place, tags, preferred_element_type=f32).astype(jnp.int32)
    send_doc, slot_plus = picked[:, 0] - 1, picked[:, 1]
    first_doc, second_doc = send_doc[: group * capacity], send_doc[group * capacity :]

    extra = 16
    doc_part = (first_doc[:, None] == jnp.arange(docs, dtype=jnp.int32)[None, :]).astype(bf16)
    doc_part = jnp.concatenate(
        [doc_part.reshape(group, capacity, docs), jnp.zeros((group, extra, docs), bf16)], axis=1
    )
    slot_row = slot_plus.astype(bf16).reshape(2, group, capacity).transpose(1, 0, 2)
    slot_row = slot_row.reshape(group, 1, 2 * capacity)
    slot_part = jnp.concatenate(
        [
            jnp.zeros((group, capacity, 2 * capacity), bf16),
            slot_row,
            jnp.zeros((group, extra - 1, 2 * capacity), bf16),
        ],
        axis=1,
    )
    chooser = jnp.concatenate([doc_part, slot_part], axis=2)
    chooser = chooser.reshape(group * (capacity + extra), docs + 2 * capacity)
    table = jnp.concatenate([doc_embed, jnp.eye(2 * capacity, width, dtype=bf16)], axis=0)
    send_first = jnp.dot(chooser, table, preferred_element_type=f32).astype(bf16)
    pick = (second_doc[:, None] == jnp.arange(docs, dtype=jnp.int32)[None, :]).astype(bf16)
    send_second = jnp.dot(pick, doc_embed, preferred_element_type=f32).astype(bf16)

    got_first = lax.all_to_all(
        send_first.reshape(group, capacity + extra, width), near, split_axis=0, concat_axis=0, tiled=True
    )
    got_second = lax.all_to_all(
        send_second.reshape(group, capacity, width), near, split_axis=0, concat_axis=0, tiled=True
    )
    slots = got_first[:, capacity, : 2 * capacity].astype(jnp.int32) - 1
    first_slot = jnp.concatenate(
        [slots[:, :capacity], jnp.full((group, extra), -1, jnp.int32)], axis=1
    ).reshape(group * (capacity + extra))
    second_slot = slots[:, capacity:].reshape(group * capacity)

    label_ids = jnp.arange(owned, dtype=jnp.int32)
    first_hot = (label_ids[:, None] == first_slot[None, :]).astype(bf16)
    mirror_part = jnp.dot(
        first_hot, got_first.reshape(group * (capacity + extra), width), preferred_element_type=f32
    )
    mirrored = lax.ppermute(mirror_part, "zh", [(0, 1), (1, 0)])
    second_hot = (label_ids[:, None] == second_slot[None, :]).astype(bf16)
    own_part = jnp.dot(
        second_hot, got_second.reshape(group * capacity, width), preferred_element_type=f32
    )
    label_sums = own_part + mirrored
    label_vectors = rms_scale(label_sums).astype(bf16)
    members = (jnp.arange(CLUSTERS, dtype=jnp.int32)[:, None] == label_cluster[None, :]).astype(bf16)
    partial_sums = jnp.dot(members, label_vectors, preferred_element_type=f32)

    if CLUSTERS % group == 0:
        chips = ("y", "zr")
        count = group // 2
        share = CLUSTERS // group
        pair = lax.all_to_all(
            partial_sums.reshape(2, CLUSTERS // 2, width), "core", split_axis=0, concat_axis=0, tiled=True
        )
        parts = lax.all_to_all(
            jnp.sum(pair, axis=0).reshape(count, share, width), chips, split_axis=0, concat_axis=0, tiled=True
        )
        half_sums = jnp.sum(parts, axis=0)
        sums = half_sums + lax.ppermute(half_sums, "zh", [(0, 1), (1, 0)])
        own = rms_scale(sums).astype(bf16)
        core_c = lax.all_to_all(
            jnp.broadcast_to(own[None], (count, share, width)), chips, split_axis=0, concat_axis=0, tiled=True
        ).reshape(CLUSTERS // 2, width)
        centroids = lax.all_to_all(
            jnp.broadcast_to(core_c[None], (2, CLUSTERS // 2, width)),
            "core",
            split_axis=0,
            concat_axis=0,
            tiled=True,
        ).reshape(CLUSTERS, width)
    else:
        centroids = rms_scale(lax.psum(partial_sums, axes)).astype(bf16)
    inner = lax.dot_general(
        label_vectors, centroids, (((1,), (1,)), ((), ())), preferred_element_type=f32
    )
    distances = 1.0 - inner / float(width)
    return (label_vectors, centroids, distances)


def solution(mesh):
    rows, cols = mesh.shape["row"], mesh.shape["col"]
    split = Mesh(mesh.devices.reshape(rows // 2, 2, 2, cols // 2), ("y", "core", "zh", "zr"))
    spread = ("y", "core", "zh", "zr")
    placed = (P(spread, None), P(spread), P(spread, None), P(spread), P(spread))
    return jax.shard_map(
        local,
        mesh=split,
        in_specs=placed,
        out_specs=(P(spread, None), P(), P(spread, None)),
        check_vma=False,
    )
```

```python
import jax
import jax.numpy as jnp
from jax import lax
from jax.sharding import Mesh, PartitionSpec as P

CLUSTERS = 256


def rms_scale(values):
    return values * lax.rsqrt(jnp.mean(values * values, axis=-1, keepdims=True) + 1e-06)


def local(doc_embed, pair_doc, pair_owner, pair_slot, label_cluster):
    axes = ("y", "core", "zh", "zr")
    near = ("y", "core", "zr")
    devices = lax.axis_size(axes)
    halves = lax.axis_size("zr")
    group = devices // 2
    pairs = pair_doc.shape[0]
    docs, width = doc_embed.shape
    owned = label_cluster.shape[0]
    capacity = 2 * pairs // devices
    owner = pair_owner[:, 0]
    f32, bf16 = jnp.float32, jnp.bfloat16

    owner_hits = (owner[:, None] == jnp.arange(devices, dtype=jnp.int32)[None, :]).astype(bf16)
    pid = jnp.arange(pairs, dtype=jnp.int32)
    earlier = (pid[None, :] < pid[:, None]).astype(bf16)
    before = jnp.dot(earlier, owner_hits, preferred_element_type=f32)
    rank = jnp.sum(before * owner_hits.astype(f32), axis=1).astype(jnp.int32)
    cols = 2 * halves
    o_row, o_col = owner // cols, owner % cols
    o_zh, o_zr = o_col // halves, o_col % halves
    proxy = o_row * halves + o_zr
    me = lax.axis_index("zh")
    later = (o_zh == me).astype(jnp.int32)
    position = later * (group * capacity) + proxy * capacity + rank

    place = (jnp.arange(devices * capacity, dtype=jnp.int32)[:, None] == position[None, :]).astype(bf16)
    tags = (jnp.stack([pair_doc, pair_slot], axis=1) + 1).astype(bf16)
    picked = jnp.dot(place, tags, preferred_element_type=f32).astype(jnp.int32)
    send_doc, slot_plus = picked[:, 0] - 1, picked[:, 1]
    first_doc, second_doc = send_doc[: group * capacity], send_doc[group * capacity :]

    lanes = 128
    wide = width + lanes
    doc_part = (first_doc[:, None] == jnp.arange(docs, dtype=jnp.int32)[None, :]).astype(bf16)
    slot_part = slot_plus.astype(bf16).reshape(2, group * capacity).T
    chooser = jnp.concatenate([doc_part, slot_part], axis=1)
    table = jnp.concatenate(
        [
            jnp.concatenate([doc_embed, jnp.zeros((docs, lanes), bf16)], axis=1),
            jnp.concatenate([jnp.zeros((2, width), bf16), jnp.eye(2, lanes, dtype=bf16)], axis=1),
        ],
        axis=0,
    )
    send_first = jnp.dot(chooser, table, preferred_element_type=f32).astype(bf16)
    pick = (second_doc[:, None] == jnp.arange(docs, dtype=jnp.int32)[None, :]).astype(bf16)
    send_second = jnp.dot(pick, doc_embed, preferred_element_type=f32).astype(bf16)

    got_first = lax.all_to_all(
        send_first.reshape(group, capacity, wide), near, split_axis=0, concat_axis=0, tiled=True
    ).reshape(group * capacity, wide)
    got_second = lax.all_to_all(
        send_second.reshape(group, capacity, width), near, split_axis=0, concat_axis=0, tiled=True
    ).reshape(group * capacity, width)
    first_slot = got_first[:, width].astype(jnp.int32) - 1
    second_slot = got_first[:, width + 1].astype(jnp.int32) - 1

    label_ids = jnp.arange(owned, dtype=jnp.int32)
    first_hot = (label_ids[:, None] == first_slot[None, :]).astype(bf16)
    mirror_part = jnp.dot(first_hot, got_first, preferred_element_type=f32)[:, :width]
    mirrored = lax.ppermute(mirror_part, "zh", [(0, 1), (1, 0)])
    second_hot = (label_ids[:, None] == second_slot[None, :]).astype(bf16)
    own_part = jnp.dot(second_hot, got_second, preferred_element_type=f32)
    label_sums = own_part + mirrored
    label_vectors = rms_scale(label_sums).astype(bf16)
    members = (jnp.arange(CLUSTERS, dtype=jnp.int32)[:, None] == label_cluster[None, :]).astype(bf16)
    partial_sums = jnp.dot(members, label_vectors, preferred_element_type=f32)

    if CLUSTERS % group == 0:
        share = CLUSTERS // group
        parts = lax.all_to_all(
            partial_sums.reshape(group, share, width), near, split_axis=0, concat_axis=0, tiled=True
        )
        half_sums = jnp.sum(parts, axis=0)
        sums = half_sums + lax.ppermute(half_sums, "zh", [(0, 1), (1, 0)])
        own = rms_scale(sums).astype(bf16)
        centroids = lax.all_to_all(
            jnp.broadcast_to(own[None], (group, share, width)),
            near,
            split_axis=0,
            concat_axis=0,
            tiled=True,
        ).reshape(CLUSTERS, width)
    else:
        centroids = rms_scale(lax.psum(partial_sums, axes)).astype(bf16)
    inner = lax.dot_general(
        label_vectors, centroids, (((1,), (1,)), ((), ())), preferred_element_type=f32
    )
    distances = 1.0 - inner / float(width)
    return (label_vectors, centroids, distances)


def solution(mesh):
    rows, cols = mesh.shape["row"], mesh.shape["col"]
    split = Mesh(mesh.devices.reshape(rows // 2, 2, 2, cols // 2), ("y", "core", "zh", "zr"))
    spread = ("y", "core", "zh", "zr")
    placed = (P(spread, None), P(spread), P(spread, None), P(spread), P(spread))
    return jax.shard_map(
        local,
        mesh=split,
        in_specs=placed,
        out_specs=(P(spread, None), P(), P(spread, None)),
        check_vma=False,
    )
```

```python
import jax
import jax.numpy as jnp
from jax import lax
from jax.sharding import Mesh, PartitionSpec as P

CLUSTERS = 256


def rms_scale(values):
    return values * lax.rsqrt(jnp.mean(values * values, axis=-1, keepdims=True) + 1e-06)


def local(doc_embed, pair_doc, pair_owner, pair_slot, label_cluster):
    axes = ("y", "core", "zh", "zr")
    near = ("y", "core", "zr")
    devices = lax.axis_size(axes)
    halves = lax.axis_size("zr")
    group = devices // 2
    pairs = pair_doc.shape[0]
    docs, width = doc_embed.shape
    owned = label_cluster.shape[0]
    capacity = 2 * pairs // devices
    owner = pair_owner[:, 0]
    f32, bf16 = jnp.float32, jnp.bfloat16

    cols = 2 * halves
    o_row, o_col = owner // cols, owner % cols
    o_zh, o_zr = o_col // halves, o_col % halves
    proxy = o_row * halves + o_zr
    me = lax.axis_index("zh")
    later = (o_zh == me).astype(jnp.int32)
    block = later * group + proxy

    chunk = 32
    hits = (block[:, None] == jnp.arange(devices, dtype=jnp.int32)[None, :]).astype(bf16)
    hits3 = hits.reshape(pairs // chunk, chunk, devices)
    step = jnp.arange(chunk, dtype=jnp.int32)
    inside = (step[None, :] < step[:, None]).astype(bf16)
    within = jnp.einsum("ij,cjo->cio", inside, hits3, preferred_element_type=f32)
    totals = jnp.sum(hits3.astype(f32), axis=1)
    lead = jnp.arange(pairs // chunk, dtype=jnp.int32)
    ahead = (lead[None, :] < lead[:, None]).astype(f32)
    offsets = jnp.dot(ahead, totals, preferred_element_type=f32)
    counts = (within + offsets[:, None, :]).reshape(pairs, devices)
    rank = jnp.sum(counts * hits.astype(f32), axis=1).astype(jnp.int32)

    at_rank = (rank[:, None] == jnp.arange(capacity, dtype=jnp.int32)[None, :]).astype(f32)
    tagged = jnp.concatenate(
        [at_rank * (pair_doc + 1).astype(f32)[:, None], at_rank * (pair_slot + 1).astype(f32)[:, None]],
        axis=1,
    ).astype(bf16)
    picked = lax.dot_general(
        hits, tagged, (((0,), (0,)), ((), ())), preferred_element_type=f32
    ).astype(jnp.int32)
    send_doc = picked[:, :capacity].reshape(devices * capacity) - 1
    slot_plus = picked[:, capacity:].reshape(devices * capacity)
    first_doc, second_doc = send_doc[: group * capacity], send_doc[group * capacity :]

    lanes = 128
    wide = width + lanes
    doc_part = (first_doc[:, None] == jnp.arange(docs, dtype=jnp.int32)[None, :]).astype(bf16)
    slot_part = slot_plus.astype(bf16).reshape(2, group * capacity).T
    chooser = jnp.concatenate([doc_part, slot_part], axis=1)
    table = jnp.concatenate(
        [
            jnp.concatenate([doc_embed, jnp.zeros((docs, lanes), bf16)], axis=1),
            jnp.concatenate([jnp.zeros((2, width), bf16), jnp.eye(2, lanes, dtype=bf16)], axis=1),
        ],
        axis=0,
    )
    send_first = jnp.dot(chooser, table, preferred_element_type=f32).astype(bf16)
    pick = (second_doc[:, None] == jnp.arange(docs, dtype=jnp.int32)[None, :]).astype(bf16)
    send_second = jnp.dot(pick, doc_embed, preferred_element_type=f32).astype(bf16)

    got_first = lax.all_to_all(
        send_first.reshape(group, capacity, wide), near, split_axis=0, concat_axis=0, tiled=True
    ).reshape(group * capacity, wide)
    got_second = lax.all_to_all(
        send_second.reshape(group, capacity, width), near, split_axis=0, concat_axis=0, tiled=True
    ).reshape(group * capacity, width)
    first_slot = got_first[:, width].astype(jnp.int32) - 1
    second_slot = got_first[:, width + 1].astype(jnp.int32) - 1

    label_ids = jnp.arange(owned, dtype=jnp.int32)
    first_hot = (label_ids[:, None] == first_slot[None, :]).astype(bf16)
    mirror_part = jnp.dot(first_hot, got_first, preferred_element_type=f32)[:, :width]
    mirrored = lax.ppermute(mirror_part, "zh", [(0, 1), (1, 0)])
    second_hot = (label_ids[:, None] == second_slot[None, :]).astype(bf16)
    own_part = jnp.dot(second_hot, got_second, preferred_element_type=f32)
    label_sums = own_part + mirrored
    label_vectors = rms_scale(label_sums).astype(bf16)
    members = (jnp.arange(CLUSTERS, dtype=jnp.int32)[:, None] == label_cluster[None, :]).astype(bf16)
    partial_sums = jnp.dot(members, label_vectors, preferred_element_type=f32)

    if CLUSTERS % group == 0:
        share = CLUSTERS // group
        parts = lax.all_to_all(
            partial_sums.reshape(group, share, width), near, split_axis=0, concat_axis=0, tiled=True
        )
        half_sums = jnp.sum(parts, axis=0)
        sums = half_sums + lax.ppermute(half_sums, "zh", [(0, 1), (1, 0)])
        own = rms_scale(sums).astype(bf16)
        centroids = lax.all_to_all(
            jnp.broadcast_to(own[None], (group, share, width)),
            near,
            split_axis=0,
            concat_axis=0,
            tiled=True,
        ).reshape(CLUSTERS, width)
    else:
        centroids = rms_scale(lax.psum(partial_sums, axes)).astype(bf16)
    inner = lax.dot_general(
        label_vectors, centroids, (((1,), (1,)), ((), ())), preferred_element_type=f32
    )
    distances = 1.0 - inner / float(width)
    return (label_vectors, centroids, distances)


def solution(mesh):
    rows, cols = mesh.shape["row"], mesh.shape["col"]
    split = Mesh(mesh.devices.reshape(rows // 2, 2, 2, cols // 2), ("y", "core", "zh", "zr"))
    spread = ("y", "core", "zh", "zr")
    placed = (P(spread, None), P(spread), P(spread, None), P(spread), P(spread))
    return jax.shard_map(
        local,
        mesh=split,
        in_specs=placed,
        out_specs=(P(spread, None), P(), P(spread, None)),
        check_vma=False,
    )
```

```python
import jax
import jax.numpy as jnp
from jax import lax
from jax.sharding import Mesh, PartitionSpec as P

CLUSTERS = 256


def rms_scale(values):
    return values * lax.rsqrt(jnp.mean(values * values, axis=-1, keepdims=True) + 1e-06)


def local(doc_embed, pair_doc, pair_owner, pair_slot, label_cluster):
    axes = ("y", "core", "zh", "zr")
    near = ("y", "core", "zr")
    devices = lax.axis_size(axes)
    halves = lax.axis_size("zr")
    group = devices // 2
    pairs = pair_doc.shape[0]
    docs, width = doc_embed.shape
    owned = label_cluster.shape[0]
    capacity = 2 * pairs // devices
    f32, bf16 = jnp.float32, jnp.bfloat16

    me = lax.axis_index("zh")
    b = jnp.arange(devices, dtype=jnp.int32)
    b_later, b_proxy = b // group, b % group
    b_zh = jnp.where(b_later == 1, me, 1 - me)
    block_owner = (b_proxy // halves) * (2 * halves) + b_zh * halves + b_proxy % halves

    chunk = 32
    hits = (pair_owner == block_owner[None, :]).astype(bf16)
    hits3 = hits.reshape(pairs // chunk, chunk, devices)
    step = jnp.arange(chunk, dtype=jnp.int32)
    inside = (step[None, :] < step[:, None]).astype(bf16)
    within = jnp.einsum("ij,cjo->cio", inside, hits3, preferred_element_type=f32)
    totals = jnp.sum(hits3.astype(f32), axis=1)
    lead = jnp.arange(pairs // chunk, dtype=jnp.int32)
    ahead = (lead[None, :] < lead[:, None]).astype(f32)
    offsets = jnp.dot(ahead, totals, preferred_element_type=f32)
    counts = (within + offsets[:, None, :]).reshape(pairs, devices)
    rank = jnp.sum(counts * hits.astype(f32), axis=1).astype(jnp.int32)

    at_rank = (rank[:, None] == jnp.arange(capacity, dtype=jnp.int32)[None, :]).astype(f32)
    tagged = jnp.concatenate(
        [at_rank * (pair_doc + 1).astype(f32)[:, None], at_rank * (pair_slot + 1).astype(f32)[:, None]],
        axis=1,
    ).astype(bf16)
    picked = lax.dot_general(
        hits, tagged, (((0,), (0,)), ((), ())), preferred_element_type=f32
    ).astype(jnp.int32)
    send_doc = picked[:, :capacity].reshape(devices * capacity) - 1
    slot_plus = picked[:, capacity:].reshape(devices * capacity)
    first_doc, second_doc = send_doc[: group * capacity], send_doc[group * capacity :]

    lanes = 128
    wide = width + lanes
    doc_part = (first_doc[:, None] == jnp.arange(docs, dtype=jnp.int32)[None, :]).astype(bf16)
    slot_part = slot_plus.astype(bf16).reshape(2, group * capacity).T
    chooser = jnp.concatenate([doc_part, slot_part], axis=1)
    table = jnp.concatenate(
        [
            jnp.concatenate([doc_embed, jnp.zeros((docs, lanes), bf16)], axis=1),
            jnp.concatenate([jnp.zeros((2, width), bf16), jnp.eye(2, lanes, dtype=bf16)], axis=1),
        ],
        axis=0,
    )
    send_first = jnp.dot(chooser, table, preferred_element_type=f32).astype(bf16)
    pick = (second_doc[:, None] == jnp.arange(docs, dtype=jnp.int32)[None, :]).astype(bf16)
    send_second = jnp.dot(pick, doc_embed, preferred_element_type=f32).astype(bf16)

    got_first = lax.all_to_all(
        send_first.reshape(group, capacity, wide), near, split_axis=0, concat_axis=0, tiled=True
    ).reshape(group * capacity, wide)
    got_second = lax.all_to_all(
        send_second.reshape(group, capacity, width), near, split_axis=0, concat_axis=0, tiled=True
    ).reshape(group * capacity, width)
    first_slot = got_first[:, width].astype(jnp.int32) - 1
    second_slot = got_first[:, width + 1].astype(jnp.int32) - 1

    label_ids = jnp.arange(owned, dtype=jnp.int32)
    first_hot = (label_ids[:, None] == first_slot[None, :]).astype(bf16)
    mirror_part = jnp.dot(first_hot, got_first, preferred_element_type=f32)[:, :width]
    mirrored = lax.ppermute(mirror_part, "zh", [(0, 1), (1, 0)])
    second_hot = (label_ids[:, None] == second_slot[None, :]).astype(bf16)
    own_part = jnp.dot(second_hot, got_second, preferred_element_type=f32)
    label_sums = own_part + mirrored
    label_vectors = rms_scale(label_sums).astype(bf16)
    members = (jnp.arange(CLUSTERS, dtype=jnp.int32)[:, None] == label_cluster[None, :]).astype(bf16)
    partial_sums = jnp.dot(members, label_vectors, preferred_element_type=f32)

    if CLUSTERS % group == 0:
        share = CLUSTERS // group
        parts = lax.all_to_all(
            partial_sums.reshape(group, share, width), near, split_axis=0, concat_axis=0, tiled=True
        )
        half_sums = jnp.sum(parts, axis=0)
        sums = half_sums + lax.ppermute(half_sums, "zh", [(0, 1), (1, 0)])
        own = rms_scale(sums).astype(bf16)
        centroids = lax.all_to_all(
            jnp.broadcast_to(own[None], (group, share, width)),
            near,
            split_axis=0,
            concat_axis=0,
            tiled=True,
        ).reshape(CLUSTERS, width)
    else:
        centroids = rms_scale(lax.psum(partial_sums, axes)).astype(bf16)
    inner = lax.dot_general(
        label_vectors, centroids, (((1,), (1,)), ((), ())), preferred_element_type=f32
    )
    distances = 1.0 - inner / float(width)
    return (label_vectors, centroids, distances)


def solution(mesh):
    rows, cols = mesh.shape["row"], mesh.shape["col"]
    split = Mesh(mesh.devices.reshape(rows // 2, 2, 2, cols // 2), ("y", "core", "zh", "zr"))
    spread = ("y", "core", "zh", "zr")
    placed = (P(spread, None), P(spread), P(spread, None), P(spread), P(spread))
    return jax.shard_map(
        local,
        mesh=split,
        in_specs=placed,
        out_specs=(P(spread, None), P(), P(spread, None)),
        check_vma=False,
    )
```

```python
import jax
import jax.numpy as jnp
from jax import lax
from jax.sharding import Mesh, PartitionSpec as P

CLUSTERS = 256


def rms_scale(values):
    return values * lax.rsqrt(jnp.mean(values * values, axis=-1, keepdims=True) + 1e-06)


def local(doc_embed, pair_doc, pair_owner, pair_slot, label_cluster):
    axes = ("y", "core", "zh", "zr")
    near = ("y", "core", "zr")
    devices = lax.axis_size(axes)
    halves = lax.axis_size("zr")
    group = devices // 2
    pairs = pair_doc.shape[0]
    docs, width = doc_embed.shape
    owned = label_cluster.shape[0]
    capacity = 2 * pairs // devices
    f32, bf16 = jnp.float32, jnp.bfloat16

    me = lax.axis_index("zh")
    b = jnp.arange(devices, dtype=jnp.int32)
    b_later, b_proxy = b // group, b % group
    b_zh = jnp.where(b_later == 1, me, 1 - me)
    block_owner = (b_proxy // halves) * (2 * halves) + b_zh * halves + b_proxy % halves

    owner_row = pair_owner.reshape(1, pairs)
    hits_t = (block_owner[:, None] == owner_row).astype(bf16)
    pid = jnp.arange(pairs, dtype=jnp.int32)
    earlier_t = (pid[:, None] < pid[None, :]).astype(bf16)
    before_t = jnp.dot(hits_t, earlier_t, preferred_element_type=f32)
    rank_row = jnp.sum(before_t * hits_t.astype(f32), axis=0, keepdims=True).astype(jnp.int32)

    at_rank_t = (jnp.arange(capacity, dtype=jnp.int32)[:, None] == rank_row).astype(f32)
    tagged_t = jnp.concatenate(
        [
            at_rank_t * (pair_doc.reshape(1, pairs) + 1).astype(f32),
            at_rank_t * (pair_slot.reshape(1, pairs) + 1).astype(f32),
        ],
        axis=0,
    ).astype(bf16)
    picked = lax.dot_general(
        hits_t, tagged_t, (((1,), (1,)), ((), ())), preferred_element_type=f32
    ).astype(jnp.int32)
    send_doc = picked[:, :capacity].reshape(devices * capacity) - 1
    slot_plus = picked[:, capacity:].reshape(devices * capacity)
    first_doc, second_doc = send_doc[: group * capacity], send_doc[group * capacity :]

    lanes = 128
    wide = width + lanes
    doc_part = (first_doc[:, None] == jnp.arange(docs, dtype=jnp.int32)[None, :]).astype(bf16)
    slot_part = slot_plus.astype(bf16).reshape(2, group * capacity).T
    chooser = jnp.concatenate([doc_part, slot_part], axis=1)
    table = jnp.concatenate(
        [
            jnp.concatenate([doc_embed, jnp.zeros((docs, lanes), bf16)], axis=1),
            jnp.concatenate([jnp.zeros((2, width), bf16), jnp.eye(2, lanes, dtype=bf16)], axis=1),
        ],
        axis=0,
    )
    send_first = jnp.dot(chooser, table, preferred_element_type=f32).astype(bf16)
    pick = (second_doc[:, None] == jnp.arange(docs, dtype=jnp.int32)[None, :]).astype(bf16)
    send_second = jnp.dot(pick, doc_embed, preferred_element_type=f32).astype(bf16)

    got_first = lax.all_to_all(
        send_first.reshape(group, capacity, wide), near, split_axis=0, concat_axis=0, tiled=True
    ).reshape(group * capacity, wide)
    got_second = lax.all_to_all(
        send_second.reshape(group, capacity, width), near, split_axis=0, concat_axis=0, tiled=True
    ).reshape(group * capacity, width)
    first_slot = got_first[:, width].astype(jnp.int32) - 1
    second_slot = got_first[:, width + 1].astype(jnp.int32) - 1

    label_ids = jnp.arange(owned, dtype=jnp.int32)
    first_hot = (label_ids[:, None] == first_slot[None, :]).astype(bf16)
    mirror_part = jnp.dot(first_hot, got_first, preferred_element_type=f32)[:, :width]
    mirrored = lax.ppermute(mirror_part, "zh", [(0, 1), (1, 0)])
    second_hot = (label_ids[:, None] == second_slot[None, :]).astype(bf16)
    own_part = jnp.dot(second_hot, got_second, preferred_element_type=f32)
    label_sums = own_part + mirrored
    label_vectors = rms_scale(label_sums).astype(bf16)
    members = (jnp.arange(CLUSTERS, dtype=jnp.int32)[:, None] == label_cluster[None, :]).astype(bf16)
    partial_sums = jnp.dot(members, label_vectors, preferred_element_type=f32)

    if CLUSTERS % group == 0:
        share = CLUSTERS // group
        parts = lax.all_to_all(
            partial_sums.reshape(group, share, width), near, split_axis=0, concat_axis=0, tiled=True
        )
        half_sums = jnp.sum(parts, axis=0)
        sums = half_sums + lax.ppermute(half_sums, "zh", [(0, 1), (1, 0)])
        own = rms_scale(sums).astype(bf16)
        centroids = lax.all_to_all(
            jnp.broadcast_to(own[None], (group, share, width)),
            near,
            split_axis=0,
            concat_axis=0,
            tiled=True,
        ).reshape(CLUSTERS, width)
    else:
        centroids = rms_scale(lax.psum(partial_sums, axes)).astype(bf16)
    inner = lax.dot_general(
        label_vectors, centroids, (((1,), (1,)), ((), ())), preferred_element_type=f32
    )
    distances = 1.0 - inner / float(width)
    return (label_vectors, centroids, distances)


def solution(mesh):
    rows, cols = mesh.shape["row"], mesh.shape["col"]
    split = Mesh(mesh.devices.reshape(rows // 2, 2, 2, cols // 2), ("y", "core", "zh", "zr"))
    spread = ("y", "core", "zh", "zr")
    placed = (P(spread, None), P(spread), P(spread, None), P(spread), P(spread))
    return jax.shard_map(
        local,
        mesh=split,
        in_specs=placed,
        out_specs=(P(spread, None), P(), P(spread, None)),
        check_vma=False,
    )
```

```python
import jax
import jax.numpy as jnp
from jax import lax
from jax.sharding import Mesh, PartitionSpec as P

CLUSTERS = 256


def rms_scale(values):
    return values * lax.rsqrt(jnp.mean(values * values, axis=-1, keepdims=True) + 1e-06)


def local(doc_embed, pair_doc, pair_owner, pair_slot, label_cluster):
    axes = ("y", "core", "zh", "zr")
    near = ("y", "core", "zr")
    devices = lax.axis_size(axes)
    halves = lax.axis_size("zr")
    group = devices // 2
    pairs = pair_doc.shape[0]
    docs, width = doc_embed.shape
    owned = label_cluster.shape[0]
    capacity = 2 * pairs // devices
    f32, bf16 = jnp.float32, jnp.bfloat16

    me = lax.axis_index("zh")
    b = jnp.arange(devices, dtype=jnp.int32)
    b_later, b_proxy = b // group, b % group
    b_zh = jnp.where(b_later == 1, me, 1 - me)
    block_owner = (b_proxy // halves) * (2 * halves) + b_zh * halves + b_proxy % halves

    owner_row = pair_owner.reshape(1, pairs)
    hits_t = (block_owner[:, None] == owner_row).astype(bf16)
    pid = jnp.arange(pairs, dtype=jnp.int32)
    earlier_t = (pid[:, None] < pid[None, :]).astype(bf16)
    before_t = jnp.dot(hits_t, earlier_t, preferred_element_type=f32)
    rank_row = jnp.sum(before_t * hits_t.astype(f32), axis=0, keepdims=True).astype(jnp.int32)

    at_rank_t = (jnp.arange(capacity, dtype=jnp.int32)[:, None] == rank_row).astype(f32)
    tagged_t = jnp.concatenate(
        [
            at_rank_t * (pair_doc.reshape(1, pairs) + 1).astype(f32),
            at_rank_t * (pair_slot.reshape(1, pairs) + 1).astype(f32),
        ],
        axis=0,
    ).astype(bf16)
    picked = lax.dot_general(
        hits_t, tagged_t, (((1,), (1,)), ((), ())), preferred_element_type=f32
    ).astype(jnp.int32)
    send_doc = picked[:, :capacity].reshape(devices * capacity) - 1
    slot_plus = picked[:, capacity:].reshape(devices * capacity)
    first_doc, second_doc = send_doc[: group * capacity], send_doc[group * capacity :]

    lanes = 128
    wide = width + lanes
    doc_part = (first_doc[:, None] == jnp.arange(docs, dtype=jnp.int32)[None, :]).astype(bf16)
    table = jnp.concatenate([doc_embed, jnp.zeros((docs, lanes), bf16)], axis=1)
    lane = jnp.arange(wide, dtype=jnp.int32)[None, :]
    slot_pair = slot_plus.astype(f32).reshape(2, group * capacity)
    slot_lanes = jnp.where(
        lane == width, slot_pair[0][:, None], jnp.where(lane == width + 1, slot_pair[1][:, None], 0.0)
    )
    send_first = (jnp.dot(doc_part, table, preferred_element_type=f32) + slot_lanes).astype(bf16)
    pick = (second_doc[:, None] == jnp.arange(docs, dtype=jnp.int32)[None, :]).astype(bf16)
    send_second = jnp.dot(pick, doc_embed, preferred_element_type=f32).astype(bf16)

    got_first = lax.all_to_all(
        send_first.reshape(group, capacity, wide), near, split_axis=0, concat_axis=0, tiled=True
    ).reshape(group * capacity, wide)
    got_second = lax.all_to_all(
        send_second.reshape(group, capacity, width), near, split_axis=0, concat_axis=0, tiled=True
    ).reshape(group * capacity, width)
    first_slot = got_first[:, width].astype(jnp.int32) - 1
    second_slot = got_first[:, width + 1].astype(jnp.int32) - 1

    label_ids = jnp.arange(owned, dtype=jnp.int32)
    first_hot = (label_ids[:, None] == first_slot[None, :]).astype(bf16)
    mirror_part = jnp.dot(first_hot, got_first, preferred_element_type=f32)[:, :width]
    mirrored = lax.ppermute(mirror_part, "zh", [(0, 1), (1, 0)])
    second_hot = (label_ids[:, None] == second_slot[None, :]).astype(bf16)
    own_part = jnp.dot(second_hot, got_second, preferred_element_type=f32)
    label_sums = own_part + mirrored
    label_vectors = rms_scale(label_sums).astype(bf16)
    members = (jnp.arange(CLUSTERS, dtype=jnp.int32)[:, None] == label_cluster[None, :]).astype(bf16)
    partial_sums = jnp.dot(members, label_vectors, preferred_element_type=f32)

    if CLUSTERS % group == 0:
        share = CLUSTERS // group
        parts = lax.all_to_all(
            partial_sums.reshape(group, share, width), near, split_axis=0, concat_axis=0, tiled=True
        )
        half_sums = jnp.sum(parts, axis=0)
        sums = half_sums + lax.ppermute(half_sums, "zh", [(0, 1), (1, 0)])
        own = rms_scale(sums).astype(bf16)
        centroids = lax.all_to_all(
            jnp.broadcast_to(own[None], (group, share, width)),
            near,
            split_axis=0,
            concat_axis=0,
            tiled=True,
        ).reshape(CLUSTERS, width)
    else:
        centroids = rms_scale(lax.psum(partial_sums, axes)).astype(bf16)
    inner = lax.dot_general(
        label_vectors, centroids, (((1,), (1,)), ((), ())), preferred_element_type=f32
    )
    distances = 1.0 - inner / float(width)
    return (label_vectors, centroids, distances)


def solution(mesh):
    rows, cols = mesh.shape["row"], mesh.shape["col"]
    split = Mesh(mesh.devices.reshape(rows // 2, 2, 2, cols // 2), ("y", "core", "zh", "zr"))
    spread = ("y", "core", "zh", "zr")
    placed = (P(spread, None), P(spread), P(spread, None), P(spread), P(spread))
    return jax.shard_map(
        local,
        mesh=split,
        in_specs=placed,
        out_specs=(P(spread, None), P(), P(spread, None)),
        check_vma=False,
    )
```

```python
import jax
import jax.numpy as jnp
from jax import lax
from jax.sharding import Mesh, PartitionSpec as P

CLUSTERS = 256


def rms_scale(values):
    return values * lax.rsqrt(jnp.mean(values * values, axis=-1, keepdims=True) + 1e-06)


def local(doc_embed, pair_doc, pair_owner, pair_slot, label_cluster):
    axes = ("y", "core", "zh", "zr")
    near = ("zr", "y", "core")
    devices = lax.axis_size(axes)
    halves = lax.axis_size("zr")
    group = devices // 2
    pairs = pair_doc.shape[0]
    docs, width = doc_embed.shape
    owned = label_cluster.shape[0]
    capacity = 2 * pairs // devices
    f32, bf16 = jnp.float32, jnp.bfloat16

    me = lax.axis_index("zh")
    b = jnp.arange(devices, dtype=jnp.int32)
    b_later, b_proxy = b // group, b % group
    b_zh = jnp.where(b_later == 1, me, 1 - me)
    rows = group // halves
    block_owner = (b_proxy % rows) * (2 * halves) + b_zh * halves + b_proxy // rows

    owner_row = pair_owner.reshape(1, pairs)
    hits_t = (block_owner[:, None] == owner_row).astype(bf16)
    pid = jnp.arange(pairs, dtype=jnp.int32)
    earlier_t = (pid[:, None] < pid[None, :]).astype(bf16)
    before_t = jnp.dot(hits_t, earlier_t, preferred_element_type=f32)
    rank_row = jnp.sum(before_t * hits_t.astype(f32), axis=0, keepdims=True).astype(jnp.int32)

    at_rank_t = (jnp.arange(capacity, dtype=jnp.int32)[:, None] == rank_row).astype(f32)
    tagged_t = jnp.concatenate(
        [
            at_rank_t * (pair_doc.reshape(1, pairs) + 1).astype(f32),
            at_rank_t * (pair_slot.reshape(1, pairs) + 1).astype(f32),
        ],
        axis=0,
    ).astype(bf16)
    picked = lax.dot_general(
        hits_t, tagged_t, (((1,), (1,)), ((), ())), preferred_element_type=f32
    ).astype(jnp.int32)
    send_doc = picked[:, :capacity].reshape(devices * capacity) - 1
    slot_plus = picked[:, capacity:].reshape(devices * capacity)
    first_doc, second_doc = send_doc[: group * capacity], send_doc[group * capacity :]

    lanes = 128
    wide = width + lanes
    doc_part = (first_doc[:, None] == jnp.arange(docs, dtype=jnp.int32)[None, :]).astype(bf16)
    table = jnp.concatenate([doc_embed, jnp.zeros((docs, lanes), bf16)], axis=1)
    lane = jnp.arange(wide, dtype=jnp.int32)[None, :]
    slot_pair = slot_plus.astype(f32).reshape(2, group * capacity)
    slot_lanes = jnp.where(
        lane == width, slot_pair[0][:, None], jnp.where(lane == width + 1, slot_pair[1][:, None], 0.0)
    )
    send_first = (jnp.dot(doc_part, table, preferred_element_type=f32) + slot_lanes).astype(bf16)
    pick = (second_doc[:, None] == jnp.arange(docs, dtype=jnp.int32)[None, :]).astype(bf16)
    send_second = jnp.dot(pick, doc_embed, preferred_element_type=f32).astype(bf16)

    got_first = lax.all_to_all(
        send_first.reshape(group, capacity, wide), near, split_axis=0, concat_axis=0, tiled=True
    ).reshape(group * capacity, wide)
    got_second = lax.all_to_all(
        send_second.reshape(group, capacity, width), near, split_axis=0, concat_axis=0, tiled=True
    ).reshape(group * capacity, width)
    first_slot = got_first[:, width].astype(jnp.int32) - 1
    second_slot = got_first[:, width + 1].astype(jnp.int32) - 1

    label_ids = jnp.arange(owned, dtype=jnp.int32)
    first_hot = (label_ids[:, None] == first_slot[None, :]).astype(bf16)
    mirror_part = jnp.dot(first_hot, got_first, preferred_element_type=f32)[:, :width]
    mirrored = lax.ppermute(mirror_part, "zh", [(0, 1), (1, 0)])
    second_hot = (label_ids[:, None] == second_slot[None, :]).astype(bf16)
    own_part = jnp.dot(second_hot, got_second, preferred_element_type=f32)
    label_sums = own_part + mirrored
    label_vectors = rms_scale(label_sums).astype(bf16)
    members = (jnp.arange(CLUSTERS, dtype=jnp.int32)[:, None] == label_cluster[None, :]).astype(bf16)
    partial_sums = jnp.dot(members, label_vectors, preferred_element_type=f32)

    if CLUSTERS % group == 0:
        share = CLUSTERS // group
        parts = lax.all_to_all(
            partial_sums.reshape(group, share, width), near, split_axis=0, concat_axis=0, tiled=True
        )
        half_sums = jnp.sum(parts, axis=0)
        sums = half_sums + lax.ppermute(half_sums, "zh", [(0, 1), (1, 0)])
        own = rms_scale(sums).astype(bf16)
        centroids = lax.all_to_all(
            jnp.broadcast_to(own[None], (group, share, width)),
            near,
            split_axis=0,
            concat_axis=0,
            tiled=True,
        ).reshape(CLUSTERS, width)
    else:
        centroids = rms_scale(lax.psum(partial_sums, axes)).astype(bf16)
    inner = lax.dot_general(
        label_vectors, centroids, (((1,), (1,)), ((), ())), preferred_element_type=f32
    )
    distances = 1.0 - inner / float(width)
    return (label_vectors, centroids, distances)


def solution(mesh):
    rows, cols = mesh.shape["row"], mesh.shape["col"]
    split = Mesh(mesh.devices.reshape(rows // 2, 2, 2, cols // 2), ("y", "core", "zh", "zr"))
    spread = ("y", "core", "zh", "zr")
    placed = (P(spread, None), P(spread), P(spread, None), P(spread), P(spread))
    return jax.shard_map(
        local,
        mesh=split,
        in_specs=placed,
        out_specs=(P(spread, None), P(), P(spread, None)),
        check_vma=False,
    )
```

```python
import jax
import jax.numpy as jnp
from jax import lax
from jax.sharding import Mesh, PartitionSpec as P

CLUSTERS = 256


def rms_scale(values):
    return values * lax.rsqrt(jnp.mean(values * values, axis=-1, keepdims=True) + 1e-06)


def local(doc_embed, pair_doc, pair_owner, pair_slot, label_cluster):
    axes = ("y", "core", "zh", "zr")
    near = ("y", "zr", "core")
    devices = lax.axis_size(axes)
    halves = lax.axis_size("zr")
    group = devices // 2
    pairs = pair_doc.shape[0]
    docs, width = doc_embed.shape
    owned = label_cluster.shape[0]
    capacity = 2 * pairs // devices
    f32, bf16 = jnp.float32, jnp.bfloat16

    me = lax.axis_index("zh")
    b = jnp.arange(devices, dtype=jnp.int32)
    b_later, b_proxy = b // group, b % group
    b_zh = jnp.where(b_later == 1, me, 1 - me)
    place = {}
    for name in reversed(near):
        size = lax.axis_size(name)
        place[name], b_proxy = b_proxy % size, b_proxy // size
    b_row = place["y"] * 2 + place["core"]
    block_owner = b_row * (2 * halves) + b_zh * halves + place["zr"]

    owner_row = pair_owner.reshape(1, pairs)
    hits_t = (block_owner[:, None] == owner_row).astype(bf16)
    pid = jnp.arange(pairs, dtype=jnp.int32)
    earlier_t = (pid[:, None] < pid[None, :]).astype(bf16)
    before_t = jnp.dot(hits_t, earlier_t, preferred_element_type=f32)
    rank_row = jnp.sum(before_t * hits_t.astype(f32), axis=0, keepdims=True).astype(jnp.int32)

    at_rank_t = (jnp.arange(capacity, dtype=jnp.int32)[:, None] == rank_row).astype(f32)
    tagged_t = jnp.concatenate(
        [
            at_rank_t * (pair_doc.reshape(1, pairs) + 1).astype(f32),
            at_rank_t * (pair_slot.reshape(1, pairs) + 1).astype(f32),
        ],
        axis=0,
    ).astype(bf16)
    picked = lax.dot_general(
        hits_t, tagged_t, (((1,), (1,)), ((), ())), preferred_element_type=f32
    ).astype(jnp.int32)
    send_doc = picked[:, :capacity].reshape(devices * capacity) - 1
    slot_plus = picked[:, capacity:].reshape(devices * capacity)
    first_doc, second_doc = send_doc[: group * capacity], send_doc[group * capacity :]

    lanes = 128
    wide = width + lanes
    doc_part = (first_doc[:, None] == jnp.arange(docs, dtype=jnp.int32)[None, :]).astype(bf16)
    table = jnp.concatenate([doc_embed, jnp.zeros((docs, lanes), bf16)], axis=1)
    lane = jnp.arange(wide, dtype=jnp.int32)[None, :]
    slot_pair = slot_plus.astype(f32).reshape(2, group * capacity)
    slot_lanes = jnp.where(
        lane == width, slot_pair[0][:, None], jnp.where(lane == width + 1, slot_pair[1][:, None], 0.0)
    )
    send_first = (jnp.dot(doc_part, table, preferred_element_type=f32) + slot_lanes).astype(bf16)
    pick = (second_doc[:, None] == jnp.arange(docs, dtype=jnp.int32)[None, :]).astype(bf16)
    send_second = jnp.dot(pick, doc_embed, preferred_element_type=f32).astype(bf16)

    got_first = lax.all_to_all(
        send_first.reshape(group, capacity, wide), near, split_axis=0, concat_axis=0, tiled=True
    ).reshape(group * capacity, wide)
    got_second = lax.all_to_all(
        send_second.reshape(group, capacity, width), near, split_axis=0, concat_axis=0, tiled=True
    ).reshape(group * capacity, width)
    first_slot = got_first[:, width].astype(jnp.int32) - 1
    second_slot = got_first[:, width + 1].astype(jnp.int32) - 1

    label_ids = jnp.arange(owned, dtype=jnp.int32)
    first_hot = (label_ids[:, None] == first_slot[None, :]).astype(bf16)
    mirror_part = jnp.dot(first_hot, got_first, preferred_element_type=f32)[:, :width]
    mirrored = lax.ppermute(mirror_part, "zh", [(0, 1), (1, 0)])
    second_hot = (label_ids[:, None] == second_slot[None, :]).astype(bf16)
    own_part = jnp.dot(second_hot, got_second, preferred_element_type=f32)
    label_sums = own_part + mirrored
    label_vectors = rms_scale(label_sums).astype(bf16)
    members = (jnp.arange(CLUSTERS, dtype=jnp.int32)[:, None] == label_cluster[None, :]).astype(bf16)
    partial_sums = jnp.dot(members, label_vectors, preferred_element_type=f32)

    if CLUSTERS % group == 0:
        share = CLUSTERS // group
        parts = lax.all_to_all(
            partial_sums.reshape(group, share, width), near, split_axis=0, concat_axis=0, tiled=True
        )
        half_sums = jnp.sum(parts, axis=0)
        sums = half_sums + lax.ppermute(half_sums, "zh", [(0, 1), (1, 0)])
        own = rms_scale(sums).astype(bf16)
        centroids = lax.all_to_all(
            jnp.broadcast_to(own[None], (group, share, width)),
            near,
            split_axis=0,
            concat_axis=0,
            tiled=True,
        ).reshape(CLUSTERS, width)
    else:
        centroids = rms_scale(lax.psum(partial_sums, axes)).astype(bf16)
    inner = lax.dot_general(
        label_vectors, centroids, (((1,), (1,)), ((), ())), preferred_element_type=f32
    )
    distances = 1.0 - inner / float(width)
    return (label_vectors, centroids, distances)


def solution(mesh):
    rows, cols = mesh.shape["row"], mesh.shape["col"]
    split = Mesh(mesh.devices.reshape(rows // 2, 2, 2, cols // 2), ("y", "core", "zh", "zr"))
    spread = ("y", "core", "zh", "zr")
    placed = (P(spread, None), P(spread), P(spread, None), P(spread), P(spread))
    return jax.shard_map(
        local,
        mesh=split,
        in_specs=placed,
        out_specs=(P(spread, None), P(), P(spread, None)),
        check_vma=False,
    )
```

```python
import jax
import jax.numpy as jnp
from jax import lax
from jax.sharding import Mesh, PartitionSpec as P

CLUSTERS = 256


def rms_scale(values):
    return values * lax.rsqrt(jnp.mean(values * values, axis=-1, keepdims=True) + 1e-06)


def local(doc_embed, pair_doc, pair_owner, pair_slot, label_cluster):
    axes = ("y", "core", "zh", "zr")
    near = ("core", "y", "zr")
    devices = lax.axis_size(axes)
    halves = lax.axis_size("zr")
    group = devices // 2
    pairs = pair_doc.shape[0]
    docs, width = doc_embed.shape
    owned = label_cluster.shape[0]
    capacity = 2 * pairs // devices
    f32, bf16 = jnp.float32, jnp.bfloat16

    me = lax.axis_index("zh")
    b = jnp.arange(devices, dtype=jnp.int32)
    b_later, b_proxy = b // group, b % group
    b_zh = jnp.where(b_later == 1, me, 1 - me)
    place = {}
    for name in reversed(near):
        size = lax.axis_size(name)
        place[name], b_proxy = b_proxy % size, b_proxy // size
    b_row = place["y"] * 2 + place["core"]
    block_owner = b_row * (2 * halves) + b_zh * halves + place["zr"]

    owner_row = pair_owner.reshape(1, pairs)
    hits_t = (block_owner[:, None] == owner_row).astype(bf16)
    pid = jnp.arange(pairs, dtype=jnp.int32)
    earlier_t = (pid[:, None] < pid[None, :]).astype(bf16)
    before_t = jnp.dot(hits_t, earlier_t, preferred_element_type=f32)
    rank_row = jnp.sum(before_t * hits_t.astype(f32), axis=0, keepdims=True).astype(jnp.int32)

    at_rank_t = (jnp.arange(capacity, dtype=jnp.int32)[:, None] == rank_row).astype(f32)
    tagged_t = jnp.concatenate(
        [
            at_rank_t * (pair_doc.reshape(1, pairs) + 1).astype(f32),
            at_rank_t * (pair_slot.reshape(1, pairs) + 1).astype(f32),
        ],
        axis=0,
    ).astype(bf16)
    picked = lax.dot_general(
        hits_t, tagged_t, (((1,), (1,)), ((), ())), preferred_element_type=f32
    ).astype(jnp.int32)
    send_doc = picked[:, :capacity].reshape(devices * capacity) - 1
    slot_plus = picked[:, capacity:].reshape(devices * capacity)
    first_doc, second_doc = send_doc[: group * capacity], send_doc[group * capacity :]

    lanes = 128
    wide = width + lanes
    doc_part = (first_doc[:, None] == jnp.arange(docs, dtype=jnp.int32)[None, :]).astype(bf16)
    table = jnp.concatenate([doc_embed, jnp.zeros((docs, lanes), bf16)], axis=1)
    lane = jnp.arange(wide, dtype=jnp.int32)[None, :]
    slot_pair = slot_plus.astype(f32).reshape(2, group * capacity)
    slot_lanes = jnp.where(
        lane == width, slot_pair[0][:, None], jnp.where(lane == width + 1, slot_pair[1][:, None], 0.0)
    )
    send_first = (jnp.dot(doc_part, table, preferred_element_type=f32) + slot_lanes).astype(bf16)
    pick = (second_doc[:, None] == jnp.arange(docs, dtype=jnp.int32)[None, :]).astype(bf16)
    send_second = jnp.dot(pick, doc_embed, preferred_element_type=f32).astype(bf16)

    got_first = lax.all_to_all(
        send_first.reshape(group, capacity, wide), near, split_axis=0, concat_axis=0, tiled=True
    ).reshape(group * capacity, wide)
    got_second = lax.all_to_all(
        send_second.reshape(group, capacity, width), near, split_axis=0, concat_axis=0, tiled=True
    ).reshape(group * capacity, width)
    first_slot = got_first[:, width].astype(jnp.int32) - 1
    second_slot = got_first[:, width + 1].astype(jnp.int32) - 1

    label_ids = jnp.arange(owned, dtype=jnp.int32)
    first_hot = (label_ids[:, None] == first_slot[None, :]).astype(bf16)
    mirror_part = jnp.dot(first_hot, got_first, preferred_element_type=f32)[:, :width]
    mirrored = lax.ppermute(mirror_part, "zh", [(0, 1), (1, 0)])
    second_hot = (label_ids[:, None] == second_slot[None, :]).astype(bf16)
    own_part = jnp.dot(second_hot, got_second, preferred_element_type=f32)
    label_sums = own_part + mirrored
    label_vectors = rms_scale(label_sums).astype(bf16)
    members = (jnp.arange(CLUSTERS, dtype=jnp.int32)[:, None] == label_cluster[None, :]).astype(bf16)
    partial_sums = jnp.dot(members, label_vectors, preferred_element_type=f32)

    if CLUSTERS % group == 0:
        share = CLUSTERS // group
        parts = lax.all_to_all(
            partial_sums.reshape(group, share, width), near, split_axis=0, concat_axis=0, tiled=True
        )
        half_sums = jnp.sum(parts, axis=0)
        sums = half_sums + lax.ppermute(half_sums, "zh", [(0, 1), (1, 0)])
        own = rms_scale(sums).astype(bf16)
        centroids = lax.all_to_all(
            jnp.broadcast_to(own[None], (group, share, width)),
            near,
            split_axis=0,
            concat_axis=0,
            tiled=True,
        ).reshape(CLUSTERS, width)
    else:
        centroids = rms_scale(lax.psum(partial_sums, axes)).astype(bf16)
    inner = lax.dot_general(
        label_vectors, centroids, (((1,), (1,)), ((), ())), preferred_element_type=f32
    )
    distances = 1.0 - inner / float(width)
    return (label_vectors, centroids, distances)


def solution(mesh):
    rows, cols = mesh.shape["row"], mesh.shape["col"]
    split = Mesh(mesh.devices.reshape(rows // 2, 2, 2, cols // 2), ("y", "core", "zh", "zr"))
    spread = ("y", "core", "zh", "zr")
    placed = (P(spread, None), P(spread), P(spread, None), P(spread), P(spread))
    return jax.shard_map(
        local,
        mesh=split,
        in_specs=placed,
        out_specs=(P(spread, None), P(), P(spread, None)),
        check_vma=False,
    )
```

```python
import jax
import jax.numpy as jnp
from jax import lax
from jax.sharding import Mesh, PartitionSpec as P

CLUSTERS = 256


def rms_scale(values):
    return values * lax.rsqrt(jnp.mean(values * values, axis=-1, keepdims=True) + 1e-06)


def local(doc_embed, pair_doc, pair_owner, pair_slot, label_cluster):
    axes = ("y", "core", "zh", "zl", "x")
    near = ("y", "core", "x", "zl")
    devices = lax.axis_size(axes)
    halves = lax.axis_size(("zl", "x"))
    group = devices // 2
    pairs = pair_doc.shape[0]
    docs, width = doc_embed.shape
    owned = label_cluster.shape[0]
    capacity = 2 * pairs // devices
    f32, bf16 = jnp.float32, jnp.bfloat16

    me = lax.axis_index("zh")
    b = jnp.arange(devices, dtype=jnp.int32)
    b_later, b_proxy = b // group, b % group
    b_zh = jnp.where(b_later == 1, me, 1 - me)
    place = {}
    for name in reversed(near):
        size = lax.axis_size(name)
        place[name], b_proxy = b_proxy % size, b_proxy // size
    b_row = place["y"] * 2 + place["core"]
    b_zr = place["zl"] * lax.axis_size("x") + place["x"]
    block_owner = b_row * (2 * halves) + b_zh * halves + b_zr

    owner_row = pair_owner.reshape(1, pairs)
    hits_t = (block_owner[:, None] == owner_row).astype(bf16)
    pid = jnp.arange(pairs, dtype=jnp.int32)
    earlier_t = (pid[:, None] < pid[None, :]).astype(bf16)
    before_t = jnp.dot(hits_t, earlier_t, preferred_element_type=f32)
    rank_row = jnp.sum(before_t * hits_t.astype(f32), axis=0, keepdims=True).astype(jnp.int32)

    at_rank_t = (jnp.arange(capacity, dtype=jnp.int32)[:, None] == rank_row).astype(f32)
    tagged_t = jnp.concatenate(
        [
            at_rank_t * (pair_doc.reshape(1, pairs) + 1).astype(f32),
            at_rank_t * (pair_slot.reshape(1, pairs) + 1).astype(f32),
        ],
        axis=0,
    ).astype(bf16)
    picked = lax.dot_general(
        hits_t, tagged_t, (((1,), (1,)), ((), ())), preferred_element_type=f32
    ).astype(jnp.int32)
    send_doc = picked[:, :capacity].reshape(devices * capacity) - 1
    slot_plus = picked[:, capacity:].reshape(devices * capacity)
    first_doc, second_doc = send_doc[: group * capacity], send_doc[group * capacity :]

    lanes = 128
    wide = width + lanes
    doc_part = (first_doc[:, None] == jnp.arange(docs, dtype=jnp.int32)[None, :]).astype(bf16)
    table = jnp.concatenate([doc_embed, jnp.zeros((docs, lanes), bf16)], axis=1)
    lane = jnp.arange(wide, dtype=jnp.int32)[None, :]
    slot_pair = slot_plus.astype(f32).reshape(2, group * capacity)
    slot_lanes = jnp.where(
        lane == width, slot_pair[0][:, None], jnp.where(lane == width + 1, slot_pair[1][:, None], 0.0)
    )
    send_first = (jnp.dot(doc_part, table, preferred_element_type=f32) + slot_lanes).astype(bf16)
    pick = (second_doc[:, None] == jnp.arange(docs, dtype=jnp.int32)[None, :]).astype(bf16)
    send_second = jnp.dot(pick, doc_embed, preferred_element_type=f32).astype(bf16)

    got_first = lax.all_to_all(
        send_first.reshape(group, capacity, wide), near, split_axis=0, concat_axis=0, tiled=True
    ).reshape(group * capacity, wide)
    got_second = lax.all_to_all(
        send_second.reshape(group, capacity, width), near, split_axis=0, concat_axis=0, tiled=True
    ).reshape(group * capacity, width)
    first_slot = got_first[:, width].astype(jnp.int32) - 1
    second_slot = got_first[:, width + 1].astype(jnp.int32) - 1

    label_ids = jnp.arange(owned, dtype=jnp.int32)
    first_hot = (label_ids[:, None] == first_slot[None, :]).astype(bf16)
    mirror_part = jnp.dot(first_hot, got_first, preferred_element_type=f32)[:, :width]
    mirrored = lax.ppermute(mirror_part, "zh", [(0, 1), (1, 0)])
    second_hot = (label_ids[:, None] == second_slot[None, :]).astype(bf16)
    own_part = jnp.dot(second_hot, got_second, preferred_element_type=f32)
    label_sums = own_part + mirrored
    label_vectors = rms_scale(label_sums).astype(bf16)
    members = (jnp.arange(CLUSTERS, dtype=jnp.int32)[:, None] == label_cluster[None, :]).astype(bf16)
    partial_sums = jnp.dot(members, label_vectors, preferred_element_type=f32)

    if CLUSTERS % group == 0:
        share = CLUSTERS // group
        parts = lax.all_to_all(
            partial_sums.reshape(group, share, width), near, split_axis=0, concat_axis=0, tiled=True
        )
        half_sums = jnp.sum(parts, axis=0)
        sums = half_sums + lax.ppermute(half_sums, "zh", [(0, 1), (1, 0)])
        own = rms_scale(sums).astype(bf16)
        centroids = lax.all_to_all(
            jnp.broadcast_to(own[None], (group, share, width)),
            near,
            split_axis=0,
            concat_axis=0,
            tiled=True,
        ).reshape(CLUSTERS, width)
    else:
        centroids = rms_scale(lax.psum(partial_sums, axes)).astype(bf16)
    inner = lax.dot_general(
        label_vectors, centroids, (((1,), (1,)), ((), ())), preferred_element_type=f32
    )
    distances = 1.0 - inner / float(width)
    return (label_vectors, centroids, distances)


def solution(mesh):
    rows, cols = mesh.shape["row"], mesh.shape["col"]
    spread = ("y", "core", "zh", "zl", "x")
    split = Mesh(mesh.devices.reshape(rows // 2, 2, 2, 2, cols // 4), spread)
    placed = (P(spread, None), P(spread), P(spread, None), P(spread), P(spread))
    return jax.shard_map(
        local,
        mesh=split,
        in_specs=placed,
        out_specs=(P(spread, None), P(), P(spread, None)),
        check_vma=False,
    )
```

```python
import jax
import jax.numpy as jnp
from jax import lax
from jax.sharding import Mesh, PartitionSpec as P

CLUSTERS = 256


def rms_scale(values):
    return values * lax.rsqrt(jnp.mean(values * values, axis=-1, keepdims=True) + 1e-06)


def local(doc_embed, pair_doc, pair_owner, pair_slot, label_cluster):
    axes = ("y", "core", "zh", "zl", "x")
    near = ("y", "core", "x", "zl")
    devices = lax.axis_size(axes)
    halves = lax.axis_size(("zl", "x"))
    group = devices // 2
    pairs = pair_doc.shape[0]
    docs, width = doc_embed.shape
    owned = label_cluster.shape[0]
    capacity = 2 * pairs // devices
    f32, bf16 = jnp.float32, jnp.bfloat16

    me = lax.axis_index("zh")
    b = jnp.arange(devices, dtype=jnp.int32)
    b_later, b_proxy = b // group, b % group
    b_zh = jnp.where(b_later == 1, me, 1 - me)
    place = {}
    for name in reversed(near):
        size = lax.axis_size(name)
        place[name], b_proxy = b_proxy % size, b_proxy // size
    b_row = place["y"] * 2 + place["core"]
    b_zr = place["zl"] * lax.axis_size("x") + place["x"]
    block_owner = b_row * (2 * halves) + b_zh * halves + b_zr

    owner_row = pair_owner.reshape(1, pairs)
    hits_t = (block_owner[:, None] == owner_row).astype(bf16)
    pid = jnp.arange(pairs, dtype=jnp.int32)
    earlier_t = (pid[:, None] < pid[None, :]).astype(bf16)
    before_t = jnp.dot(hits_t, earlier_t, preferred_element_type=f32)
    rank_row = jnp.sum(before_t * hits_t.astype(f32), axis=0, keepdims=True).astype(jnp.int32)

    at_rank_t = (jnp.arange(capacity, dtype=jnp.int32)[:, None] == rank_row).astype(f32)
    tagged_t = jnp.concatenate(
        [
            at_rank_t * (pair_doc.reshape(1, pairs) + 1).astype(f32),
            at_rank_t * (pair_slot.reshape(1, pairs) + 1).astype(f32),
        ],
        axis=0,
    ).astype(bf16)
    picked = lax.dot_general(
        hits_t, tagged_t, (((1,), (1,)), ((), ())), preferred_element_type=f32
    ).astype(jnp.int32)
    send_doc = picked[:, :capacity].reshape(devices * capacity) - 1
    slot_plus = picked[:, capacity:].reshape(devices * capacity)
    first_doc, second_doc = send_doc[: group * capacity], send_doc[group * capacity :]

    lanes = 128
    wide = width + lanes
    table = jnp.concatenate([doc_embed, jnp.zeros((1, width), bf16)], axis=0)
    table_wide = jnp.concatenate([table, jnp.zeros((docs + 1, lanes), bf16)], axis=1)
    first_at = jnp.where(first_doc >= 0, first_doc, docs)
    second_at = jnp.where(second_doc >= 0, second_doc, docs)
    lane = jnp.arange(wide, dtype=jnp.int32)[None, :]
    slot_pair = slot_plus.astype(bf16).reshape(2, group * capacity)
    zero = jnp.zeros((), bf16)
    slot_lanes = jnp.where(
        lane == width, slot_pair[0][:, None], jnp.where(lane == width + 1, slot_pair[1][:, None], zero)
    )
    send_first = jnp.take(table_wide, first_at, axis=0) + slot_lanes
    send_second = jnp.take(table, second_at, axis=0)

    got_first = lax.all_to_all(
        send_first.reshape(group, capacity, wide), near, split_axis=0, concat_axis=0, tiled=True
    ).reshape(group * capacity, wide)
    got_second = lax.all_to_all(
        send_second.reshape(group, capacity, width), near, split_axis=0, concat_axis=0, tiled=True
    ).reshape(group * capacity, width)
    first_slot = got_first[:, width].astype(jnp.int32) - 1
    second_slot = got_first[:, width + 1].astype(jnp.int32) - 1

    label_ids = jnp.arange(owned, dtype=jnp.int32)
    first_hot = (label_ids[:, None] == first_slot[None, :]).astype(bf16)
    mirror_part = jnp.dot(first_hot, got_first, preferred_element_type=f32)[:, :width]
    mirrored = lax.ppermute(mirror_part, "zh", [(0, 1), (1, 0)])
    second_hot = (label_ids[:, None] == second_slot[None, :]).astype(bf16)
    own_part = jnp.dot(second_hot, got_second, preferred_element_type=f32)
    label_sums = own_part + mirrored
    label_vectors = rms_scale(label_sums).astype(bf16)
    members = (jnp.arange(CLUSTERS, dtype=jnp.int32)[:, None] == label_cluster[None, :]).astype(bf16)
    partial_sums = jnp.dot(members, label_vectors, preferred_element_type=f32)

    if CLUSTERS % group == 0:
        share = CLUSTERS // group
        parts = lax.all_to_all(
            partial_sums.reshape(group, share, width), near, split_axis=0, concat_axis=0, tiled=True
        )
        half_sums = jnp.sum(parts, axis=0)
        sums = half_sums + lax.ppermute(half_sums, "zh", [(0, 1), (1, 0)])
        own = rms_scale(sums).astype(bf16)
        centroids = lax.all_to_all(
            jnp.broadcast_to(own[None], (group, share, width)),
            near,
            split_axis=0,
            concat_axis=0,
            tiled=True,
        ).reshape(CLUSTERS, width)
    else:
        centroids = rms_scale(lax.psum(partial_sums, axes)).astype(bf16)
    inner = lax.dot_general(
        label_vectors, centroids, (((1,), (1,)), ((), ())), preferred_element_type=f32
    )
    distances = 1.0 - inner / float(width)
    return (label_vectors, centroids, distances)


def solution(mesh):
    rows, cols = mesh.shape["row"], mesh.shape["col"]
    spread = ("y", "core", "zh", "zl", "x")
    split = Mesh(mesh.devices.reshape(rows // 2, 2, 2, 2, cols // 4), spread)
    placed = (P(spread, None), P(spread), P(spread, None), P(spread), P(spread))
    return jax.shard_map(
        local,
        mesh=split,
        in_specs=placed,
        out_specs=(P(spread, None), P(), P(spread, None)),
        check_vma=False,
    )
```

```python
import jax
import jax.numpy as jnp
from jax import lax
from jax.sharding import Mesh, PartitionSpec as P

CLUSTERS = 256


def rms_scale(values):
    return values * lax.rsqrt(jnp.mean(values * values, axis=-1, keepdims=True) + 1e-06)


def local(doc_embed, pair_doc, pair_owner, pair_slot, label_cluster):
    axes = ("y", "core", "zh", "zl", "x")
    near = ("y", "core", "x", "zl")
    devices = lax.axis_size(axes)
    halves = lax.axis_size(("zl", "x"))
    group = devices // 2
    pairs = pair_doc.shape[0]
    docs, width = doc_embed.shape
    owned = label_cluster.shape[0]
    capacity = 2 * pairs // devices
    f32, bf16 = jnp.float32, jnp.bfloat16

    me = lax.axis_index("zh")
    b = jnp.arange(devices, dtype=jnp.int32)
    b_later, b_proxy = b // group, b % group
    b_zh = jnp.where(b_later == 1, me, 1 - me)
    place = {}
    for name in reversed(near):
        size = lax.axis_size(name)
        place[name], b_proxy = b_proxy % size, b_proxy // size
    b_row = place["y"] * 2 + place["core"]
    b_zr = place["zl"] * lax.axis_size("x") + place["x"]
    block_owner = b_row * (2 * halves) + b_zh * halves + b_zr

    owner_row = pair_owner.reshape(1, pairs)
    hits_t = (block_owner[:, None] == owner_row).astype(bf16)
    pid = jnp.arange(pairs, dtype=jnp.int32)
    earlier_t = (pid[:, None] < pid[None, :]).astype(bf16)
    before_t = jnp.dot(hits_t, earlier_t, preferred_element_type=f32)
    rank_row = jnp.sum(before_t * hits_t.astype(f32), axis=0, keepdims=True).astype(jnp.int32)

    at_rank_t = (jnp.arange(capacity, dtype=jnp.int32)[:, None] == rank_row).astype(f32)
    tagged_t = jnp.concatenate(
        [
            at_rank_t * (pair_doc.reshape(1, pairs) + 1).astype(f32),
            at_rank_t * (pair_slot.reshape(1, pairs) + 1).astype(f32),
        ],
        axis=0,
    ).astype(bf16)
    picked = lax.dot_general(
        hits_t, tagged_t, (((1,), (1,)), ((), ())), preferred_element_type=f32
    ).astype(jnp.int32)
    send_doc = picked[:, :capacity].reshape(devices * capacity) - 1
    slot_plus = picked[:, capacity:].reshape(devices * capacity)
    first_doc, second_doc = send_doc[: group * capacity], send_doc[group * capacity :]

    lanes = 128
    wide = width + lanes
    doc_part = (first_doc[:, None] == jnp.arange(docs, dtype=jnp.int32)[None, :]).astype(bf16)
    slot_part = slot_plus.astype(bf16).reshape(2, group * capacity).T
    chooser = jnp.concatenate([doc_part, slot_part], axis=1)
    table = jnp.concatenate(
        [
            jnp.concatenate([doc_embed, jnp.zeros((docs, lanes), bf16)], axis=1),
            jnp.concatenate([jnp.zeros((2, width), bf16), jnp.eye(2, lanes, dtype=bf16)], axis=1),
        ],
        axis=0,
    )
    send_first = jnp.dot(chooser, table, preferred_element_type=f32).astype(bf16)
    pick = (second_doc[:, None] == jnp.arange(docs, dtype=jnp.int32)[None, :]).astype(bf16)
    send_second = jnp.dot(pick, doc_embed, preferred_element_type=f32).astype(bf16)

    got_first = lax.all_to_all(
        send_first.reshape(group, capacity, wide), near, split_axis=0, concat_axis=0, tiled=True
    ).reshape(group * capacity, wide)
    got_second = lax.all_to_all(
        send_second.reshape(group, capacity, width), near, split_axis=0, concat_axis=0, tiled=True
    ).reshape(group * capacity, width)
    first_slot = got_first[:, width].astype(jnp.int32) - 1
    second_slot = got_first[:, width + 1].astype(jnp.int32) - 1

    label_ids = jnp.arange(owned, dtype=jnp.int32)
    first_hot = (label_ids[:, None] == first_slot[None, :]).astype(bf16)
    mirror_part = jnp.dot(first_hot, got_first[:, :width], preferred_element_type=f32)
    mirrored = lax.ppermute(mirror_part, "zh", [(0, 1), (1, 0)])
    second_hot = (label_ids[:, None] == second_slot[None, :]).astype(bf16)
    own_part = jnp.dot(second_hot, got_second, preferred_element_type=f32)
    label_sums = own_part + mirrored
    label_vectors = rms_scale(label_sums).astype(bf16)
    members = (jnp.arange(CLUSTERS, dtype=jnp.int32)[:, None] == label_cluster[None, :]).astype(bf16)
    partial_sums = jnp.dot(members, label_vectors, preferred_element_type=f32)

    if CLUSTERS % group == 0:
        share = CLUSTERS // group
        parts = lax.all_to_all(
            partial_sums.reshape(group, share, width), near, split_axis=0, concat_axis=0, tiled=True
        )
        half_sums = jnp.sum(parts, axis=0)
        sums = half_sums + lax.ppermute(half_sums, "zh", [(0, 1), (1, 0)])
        own = rms_scale(sums).astype(bf16)
        centroids = lax.all_to_all(
            jnp.broadcast_to(own[None], (group, share, width)),
            near,
            split_axis=0,
            concat_axis=0,
            tiled=True,
        ).reshape(CLUSTERS, width)
    else:
        centroids = rms_scale(lax.psum(partial_sums, axes)).astype(bf16)
    inner = lax.dot_general(
        label_vectors, centroids, (((1,), (1,)), ((), ())), preferred_element_type=f32
    )
    distances = 1.0 - inner / float(width)
    return (label_vectors, centroids, distances)


def solution(mesh):
    rows, cols = mesh.shape["row"], mesh.shape["col"]
    spread = ("y", "core", "zh", "zl", "x")
    split = Mesh(mesh.devices.reshape(rows // 2, 2, 2, 2, cols // 4), spread)
    placed = (P(spread, None), P(spread), P(spread, None), P(spread), P(spread))
    return jax.shard_map(
        local,
        mesh=split,
        in_specs=placed,
        out_specs=(P(spread, None), P(), P(spread, None)),
        check_vma=False,
    )
```

```python
import jax
import jax.numpy as jnp
from jax import lax
from jax.sharding import Mesh, PartitionSpec as P

CLUSTERS = 256


def rms_scale(values):
    return values * lax.rsqrt(jnp.mean(values * values, axis=-1, keepdims=True) + 1e-06)


def local(doc_embed, pair_doc, pair_owner, pair_slot, label_cluster):
    axes = ("y", "core", "zh", "zl", "x")
    near = ("y", "core", "x", "zl")
    devices = lax.axis_size(axes)
    halves = lax.axis_size(("zl", "x"))
    group = devices // 2
    pairs = pair_doc.shape[0]
    docs, width = doc_embed.shape
    owned = label_cluster.shape[0]
    capacity = 2 * pairs // devices
    f32, bf16 = jnp.float32, jnp.bfloat16

    me = lax.axis_index("zh")
    b = jnp.arange(devices, dtype=jnp.int32)
    b_later, b_proxy = b // group, b % group
    b_zh = jnp.where(b_later == 1, me, 1 - me)
    place = {}
    for name in reversed(near):
        size = lax.axis_size(name)
        place[name], b_proxy = b_proxy % size, b_proxy // size
    b_row = place["y"] * 2 + place["core"]
    b_zr = place["zl"] * lax.axis_size("x") + place["x"]
    block_owner = b_row * (2 * halves) + b_zh * halves + b_zr

    owner_row = pair_owner.reshape(1, pairs)
    hits_t = (block_owner[:, None] == owner_row).astype(bf16)
    pid = jnp.arange(pairs, dtype=jnp.int32)
    earlier_t = (pid[:, None] < pid[None, :]).astype(bf16)
    before_t = jnp.dot(hits_t, earlier_t, preferred_element_type=f32)
    rank_row = jnp.sum(before_t * hits_t.astype(f32), axis=0, keepdims=True).astype(jnp.int32)

    at_rank_t = (jnp.arange(capacity, dtype=jnp.int32)[:, None] == rank_row).astype(f32)
    tagged_t = jnp.concatenate(
        [
            at_rank_t * (pair_doc.reshape(1, pairs) + 1).astype(f32),
            at_rank_t * (pair_slot.reshape(1, pairs) + 1).astype(f32),
        ],
        axis=0,
    ).astype(bf16)
    picked = lax.dot_general(
        hits_t, tagged_t, (((1,), (1,)), ((), ())), preferred_element_type=f32
    ).astype(jnp.int32)
    send_doc = picked[:, :capacity].reshape(devices * capacity) - 1
    slot_plus = picked[:, capacity:].reshape(devices * capacity)
    first_doc, second_doc = send_doc[: group * capacity], send_doc[group * capacity :]

    lanes = 128
    wide = width + lanes
    doc_part = (first_doc[:, None] == jnp.arange(docs, dtype=jnp.int32)[None, :]).astype(bf16)
    table = jnp.concatenate([doc_embed, jnp.zeros((docs, lanes), bf16)], axis=1)
    lane = jnp.arange(wide, dtype=jnp.int32)[None, :]
    slot_pair = slot_plus.astype(f32).reshape(2, group * capacity)
    slot_lanes = jnp.where(
        lane == width, slot_pair[0][:, None], jnp.where(lane == width + 1, slot_pair[1][:, None], 0.0)
    )
    send_first = (jnp.dot(doc_part, table, preferred_element_type=f32) + slot_lanes).astype(bf16)
    pick = (second_doc[:, None] == jnp.arange(docs, dtype=jnp.int32)[None, :]).astype(bf16)
    send_second = jnp.dot(pick, doc_embed, preferred_element_type=f32).astype(bf16)

    got_first = lax.all_to_all(
        send_first.reshape(group, capacity, wide), near, split_axis=0, concat_axis=0, tiled=True
    ).reshape(group * capacity, wide)
    got_second = lax.all_to_all(
        send_second.reshape(group, capacity, width), near, split_axis=0, concat_axis=0, tiled=True
    ).reshape(group * capacity, width)
    first_slot = got_first[:, width].astype(jnp.int32) - 1
    second_slot = got_first[:, width + 1].astype(jnp.int32) - 1

    label_ids = jnp.arange(owned, dtype=jnp.int32)
    first_hot = (label_ids[:, None] == first_slot[None, :]).astype(bf16)
    mirror_part = jnp.dot(first_hot, got_first, preferred_element_type=f32)[:, :width]
    mirrored = lax.ppermute(mirror_part, "zh", [(0, 1), (1, 0)])
    second_hot = (label_ids[:, None] == second_slot[None, :]).astype(bf16)
    own_part = jnp.dot(second_hot, got_second, preferred_element_type=f32)
    label_sums = own_part + mirrored
    label_vectors = rms_scale(label_sums).astype(bf16)
    members = (jnp.arange(CLUSTERS, dtype=jnp.int32)[:, None] == label_cluster[None, :]).astype(bf16)
    partial_sums = jnp.dot(members, label_vectors, preferred_element_type=f32)

    if CLUSTERS % group == 0:
        share = CLUSTERS // group
        parts = lax.all_to_all(
            partial_sums.reshape(group, share, width), near, split_axis=0, concat_axis=0, tiled=True
        )
        half_sums = jnp.sum(parts, axis=0)
        both = lax.all_to_all(
            jnp.broadcast_to(half_sums[None], (2, share, width)), "zh", split_axis=0, concat_axis=0, tiled=True
        )
        sums = both[0] + both[1]
        own = rms_scale(sums).astype(bf16)
        centroids = lax.all_to_all(
            jnp.broadcast_to(own[None], (group, share, width)),
            near,
            split_axis=0,
            concat_axis=0,
            tiled=True,
        ).reshape(CLUSTERS, width)
    else:
        centroids = rms_scale(lax.psum(partial_sums, axes)).astype(bf16)
    inner = lax.dot_general(
        label_vectors, centroids, (((1,), (1,)), ((), ())), preferred_element_type=f32
    )
    distances = 1.0 - inner / float(width)
    return (label_vectors, centroids, distances)


def solution(mesh):
    rows, cols = mesh.shape["row"], mesh.shape["col"]
    spread = ("y", "core", "zh", "zl", "x")
    split = Mesh(mesh.devices.reshape(rows // 2, 2, 2, 2, cols // 4), spread)
    placed = (P(spread, None), P(spread), P(spread, None), P(spread), P(spread))
    return jax.shard_map(
        local,
        mesh=split,
        in_specs=placed,
        out_specs=(P(spread, None), P(), P(spread, None)),
        check_vma=False,
    )
```

```python
import jax
import jax.numpy as jnp
from jax import lax
from jax.sharding import Mesh, PartitionSpec as P

CLUSTERS = 256


def rms_scale(values):
    return values * lax.rsqrt(jnp.mean(values * values, axis=-1, keepdims=True) + 1e-06)


def local(doc_embed, pair_doc, pair_owner, pair_slot, label_cluster):
    axes = ("y", "core", "zh", "zl", "x")
    near = ("y", "core", "x", "zl")
    devices = lax.axis_size(axes)
    halves = lax.axis_size(("zl", "x"))
    group = devices // 2
    pairs = pair_doc.shape[0]
    docs, width = doc_embed.shape
    owned = label_cluster.shape[0]
    capacity = 2 * pairs // devices
    f32, bf16 = jnp.float32, jnp.bfloat16

    me = lax.axis_index("zh")
    b = jnp.arange(devices, dtype=jnp.int32)
    b_later, b_proxy = b // group, b % group
    b_zh = jnp.where(b_later == 1, me, 1 - me)
    place = {}
    for name in reversed(near):
        size = lax.axis_size(name)
        place[name], b_proxy = b_proxy % size, b_proxy // size
    b_row = place["y"] * 2 + place["core"]
    b_zr = place["zl"] * lax.axis_size("x") + place["x"]
    block_owner = b_row * (2 * halves) + b_zh * halves + b_zr

    owner_row = pair_owner.reshape(1, pairs)
    hits_t = (block_owner[:, None] == owner_row).astype(bf16)
    pid = jnp.arange(pairs, dtype=jnp.int32)
    earlier_t = (pid[:, None] < pid[None, :]).astype(bf16)
    before_t = jnp.dot(hits_t, earlier_t, preferred_element_type=f32)
    rank_row = jnp.sum(before_t * hits_t.astype(f32), axis=0, keepdims=True).astype(jnp.int32)

    at_rank_t = (jnp.arange(capacity, dtype=jnp.int32)[:, None] == rank_row).astype(bf16)
    hits_f = hits_t.astype(f32)
    tagged_t = jnp.concatenate(
        [
            hits_f * (pair_doc.reshape(1, pairs) + 1).astype(f32),
            hits_f * (pair_slot.reshape(1, pairs) + 1).astype(f32),
        ],
        axis=0,
    ).astype(bf16)
    picked = lax.dot_general(
        tagged_t, at_rank_t, (((1,), (1,)), ((), ())), preferred_element_type=f32
    ).astype(jnp.int32)
    send_doc = picked[:devices].reshape(devices * capacity) - 1
    slot_plus = picked[devices:].reshape(devices * capacity)
    first_doc, second_doc = send_doc[: group * capacity], send_doc[group * capacity :]

    lanes = 128
    wide = width + lanes
    doc_part = (first_doc[:, None] == jnp.arange(docs, dtype=jnp.int32)[None, :]).astype(bf16)
    table = jnp.concatenate([doc_embed, jnp.zeros((docs, lanes), bf16)], axis=1)
    lane = jnp.arange(wide, dtype=jnp.int32)[None, :]
    slot_pair = slot_plus.astype(f32).reshape(2, group * capacity)
    slot_lanes = jnp.where(
        lane == width, slot_pair[0][:, None], jnp.where(lane == width + 1, slot_pair[1][:, None], 0.0)
    )
    send_first = (jnp.dot(doc_part, table, preferred_element_type=f32) + slot_lanes).astype(bf16)
    pick = (second_doc[:, None] == jnp.arange(docs, dtype=jnp.int32)[None, :]).astype(bf16)
    send_second = jnp.dot(pick, doc_embed, preferred_element_type=f32).astype(bf16)

    got_first = lax.all_to_all(
        send_first.reshape(group, capacity, wide), near, split_axis=0, concat_axis=0, tiled=True
    ).reshape(group * capacity, wide)
    got_second = lax.all_to_all(
        send_second.reshape(group, capacity, width), near, split_axis=0, concat_axis=0, tiled=True
    ).reshape(group * capacity, width)
    first_slot = got_first[:, width].astype(jnp.int32) - 1
    second_slot = got_first[:, width + 1].astype(jnp.int32) - 1

    label_ids = jnp.arange(owned, dtype=jnp.int32)
    first_hot = (label_ids[:, None] == first_slot[None, :]).astype(bf16)
    mirror_part = jnp.dot(first_hot, got_first, preferred_element_type=f32)[:, :width]
    mirrored = lax.ppermute(mirror_part, "zh", [(0, 1), (1, 0)])
    second_hot = (label_ids[:, None] == second_slot[None, :]).astype(bf16)
    own_part = jnp.dot(second_hot, got_second, preferred_element_type=f32)
    label_sums = own_part + mirrored
    label_vectors = rms_scale(label_sums).astype(bf16)
    members = (jnp.arange(CLUSTERS, dtype=jnp.int32)[:, None] == label_cluster[None, :]).astype(bf16)
    partial_sums = jnp.dot(members, label_vectors, preferred_element_type=f32)

    if CLUSTERS % group == 0:
        share = CLUSTERS // group
        parts = lax.all_to_all(
            partial_sums.reshape(group, share, width), near, split_axis=0, concat_axis=0, tiled=True
        )
        half_sums = jnp.sum(parts, axis=0)
        sums = half_sums + lax.ppermute(half_sums, "zh", [(0, 1), (1, 0)])
        own = rms_scale(sums).astype(bf16)
        centroids = lax.all_to_all(
            jnp.broadcast_to(own[None], (group, share, width)),
            near,
            split_axis=0,
            concat_axis=0,
            tiled=True,
        ).reshape(CLUSTERS, width)
    else:
        centroids = rms_scale(lax.psum(partial_sums, axes)).astype(bf16)
    inner = lax.dot_general(
        label_vectors, centroids, (((1,), (1,)), ((), ())), preferred_element_type=f32
    )
    distances = 1.0 - inner / float(width)
    return (label_vectors, centroids, distances)


def solution(mesh):
    rows, cols = mesh.shape["row"], mesh.shape["col"]
    spread = ("y", "core", "zh", "zl", "x")
    split = Mesh(mesh.devices.reshape(rows // 2, 2, 2, 2, cols // 4), spread)
    placed = (P(spread, None), P(spread), P(spread, None), P(spread), P(spread))
    return jax.shard_map(
        local,
        mesh=split,
        in_specs=placed,
        out_specs=(P(spread, None), P(), P(spread, None)),
        check_vma=False,
    )
```

```python
import jax
import jax.numpy as jnp
from jax import lax
from jax.sharding import Mesh, PartitionSpec as P

CLUSTERS = 256


def rms_scale(values):
    return values * lax.rsqrt(jnp.mean(values * values, axis=-1, keepdims=True) + 1e-06)


def local(doc_embed, pair_doc, pair_owner, pair_slot, label_cluster):
    axes = ("y", "core", "zh", "zl", "x")
    near = ("y", "core", "x", "zl")
    devices = lax.axis_size(axes)
    halves = lax.axis_size(("zl", "x"))
    group = devices // 2
    pairs = pair_doc.shape[0]
    docs, width = doc_embed.shape
    owned = label_cluster.shape[0]
    capacity = 2 * pairs // devices
    f32, bf16 = jnp.float32, jnp.bfloat16

    me = lax.axis_index("zh")
    b = jnp.arange(devices, dtype=jnp.int32)
    b_later, b_proxy = b // group, b % group
    b_zh = jnp.where(b_later == 1, me, 1 - me)
    place = {}
    for name in reversed(near):
        size = lax.axis_size(name)
        place[name], b_proxy = b_proxy % size, b_proxy // size
    b_row = place["y"] * 2 + place["core"]
    b_zr = place["zl"] * lax.axis_size("x") + place["x"]
    block_owner = b_row * (2 * halves) + b_zh * halves + b_zr

    owner_row = pair_owner.reshape(1, pairs)
    hits_t = (block_owner[:, None] == owner_row).astype(bf16)
    pid = jnp.arange(pairs, dtype=jnp.int32)
    earlier_t = (pid[:, None] < pid[None, :]).astype(bf16)
    before_t = jnp.dot(hits_t, earlier_t, preferred_element_type=f32)
    rank_row = jnp.sum(before_t * hits_t.astype(f32), axis=0, keepdims=True).astype(jnp.int32)

    at_rank_t = (jnp.arange(capacity, dtype=jnp.int32)[:, None] == rank_row).astype(bf16)
    hits_f = hits_t.astype(f32)
    tagged_t = jnp.concatenate(
        [
            hits_f * (pair_doc.reshape(1, pairs) + 1).astype(f32),
            hits_f * (pair_slot.reshape(1, pairs) + 1).astype(f32),
        ],
        axis=0,
    ).astype(bf16)
    picked = lax.dot_general(
        tagged_t, at_rank_t, (((1,), (1,)), ((), ())), preferred_element_type=f32
    ).astype(jnp.int32)
    send_doc = picked[:devices].reshape(devices * capacity) - 1
    slot_plus = picked[devices:].reshape(devices * capacity)
    first_doc, second_doc = send_doc[: group * capacity], send_doc[group * capacity :]

    lanes = 128
    wide = width + lanes
    doc_part = (first_doc[:, None] == jnp.arange(docs, dtype=jnp.int32)[None, :]).astype(bf16)
    table = jnp.concatenate([doc_embed, jnp.zeros((docs, lanes), bf16)], axis=1)
    lane = jnp.arange(wide, dtype=jnp.int32)[None, :]
    slot_pair = slot_plus.astype(f32).reshape(2, group * capacity)
    slot_lanes = jnp.where(
        lane == width, slot_pair[0][:, None], jnp.where(lane == width + 1, slot_pair[1][:, None], 0.0)
    )
    send_first = (jnp.dot(doc_part, table, preferred_element_type=f32) + slot_lanes).astype(bf16)
    pick = (second_doc[:, None] == jnp.arange(docs, dtype=jnp.int32)[None, :]).astype(bf16)
    send_second = jnp.dot(pick, doc_embed, preferred_element_type=f32).astype(bf16)

    got_first = lax.all_to_all(
        send_first.reshape(group, capacity, wide), near, split_axis=0, concat_axis=0, tiled=True
    ).reshape(group * capacity, wide)
    got_second = lax.all_to_all(
        send_second.reshape(group, capacity, width), near, split_axis=0, concat_axis=0, tiled=True
    ).reshape(group * capacity, width)
    first_slot = got_first[:, width].astype(jnp.int32) - 1
    second_slot = got_first[:, width + 1].astype(jnp.int32) - 1

    label_ids = jnp.arange(owned, dtype=jnp.int32)
    first_hot = (label_ids[:, None] == first_slot[None, :]).astype(bf16)
    mirror_part = jnp.dot(first_hot, got_first[:, :width], preferred_element_type=f32)
    mirrored = lax.ppermute(mirror_part, "zh", [(0, 1), (1, 0)])
    second_hot = (label_ids[:, None] == second_slot[None, :]).astype(bf16)
    own_part = jnp.dot(second_hot, got_second, preferred_element_type=f32)
    label_sums = own_part + mirrored
    label_vectors = rms_scale(label_sums).astype(bf16)
    members = (jnp.arange(CLUSTERS, dtype=jnp.int32)[:, None] == label_cluster[None, :]).astype(bf16)
    partial_sums = jnp.dot(members, label_vectors, preferred_element_type=f32)

    if CLUSTERS % group == 0:
        share = CLUSTERS // group
        parts = lax.all_to_all(
            partial_sums.reshape(group, share, width), near, split_axis=0, concat_axis=0, tiled=True
        )
        half_sums = jnp.sum(parts, axis=0)
        sums = half_sums + lax.ppermute(half_sums, "zh", [(0, 1), (1, 0)])
        own = rms_scale(sums).astype(bf16)
        centroids = lax.all_to_all(
            jnp.broadcast_to(own[None], (group, share, width)),
            near,
            split_axis=0,
            concat_axis=0,
            tiled=True,
        ).reshape(CLUSTERS, width)
    else:
        centroids = rms_scale(lax.psum(partial_sums, axes)).astype(bf16)
    inner = lax.dot_general(
        label_vectors, centroids, (((1,), (1,)), ((), ())), preferred_element_type=f32
    )
    distances = 1.0 - inner / float(width)
    return (label_vectors, centroids, distances)


def solution(mesh):
    rows, cols = mesh.shape["row"], mesh.shape["col"]
    spread = ("y", "core", "zh", "zl", "x")
    split = Mesh(mesh.devices.reshape(rows // 2, 2, 2, 2, cols // 4), spread)
    placed = (P(spread, None), P(spread), P(spread, None), P(spread), P(spread))
    return jax.shard_map(
        local,
        mesh=split,
        in_specs=placed,
        out_specs=(P(spread, None), P(), P(spread, None)),
        check_vma=False,
    )
```

```python
import jax
import jax.numpy as jnp
from jax import lax
from jax.sharding import Mesh, PartitionSpec as P

CLUSTERS = 256


def rms_scale(values):
    return values * lax.rsqrt(jnp.mean(values * values, axis=-1, keepdims=True) + 1e-06)


def local(doc_embed, pair_doc, pair_owner, pair_slot, label_cluster):
    axes = ("y", "core", "zh", "zl", "x")
    near = ("y", "core", "x", "zl")
    devices = lax.axis_size(axes)
    halves = lax.axis_size(("zl", "x"))
    group = devices // 2
    pairs = pair_doc.shape[0]
    docs, width = doc_embed.shape
    owned = label_cluster.shape[0]
    capacity = 2 * pairs // devices
    f32, bf16 = jnp.float32, jnp.bfloat16

    me = lax.axis_index("zh")
    b = jnp.arange(devices, dtype=jnp.int32)
    b_later, b_proxy = b // group, b % group
    b_zh = jnp.where(b_later == 1, me, 1 - me)
    place = {}
    for name in reversed(near):
        size = lax.axis_size(name)
        place[name], b_proxy = b_proxy % size, b_proxy // size
    b_row = place["y"] * 2 + place["core"]
    b_zr = place["zl"] * lax.axis_size("x") + place["x"]
    block_owner = b_row * (2 * halves) + b_zh * halves + b_zr

    owner_row = pair_owner.reshape(1, pairs)
    hits_t = (block_owner[:, None] == owner_row).astype(bf16)
    pid = jnp.arange(pairs, dtype=jnp.int32)
    earlier_t = (pid[:, None] < pid[None, :]).astype(bf16)
    before_t = jnp.dot(hits_t, earlier_t, preferred_element_type=f32)
    rank_row = jnp.sum(before_t * hits_t.astype(f32), axis=0, keepdims=True).astype(jnp.int32)

    at_rank_t = (jnp.arange(capacity, dtype=jnp.int32)[:, None] == rank_row).astype(f32)
    tagged_t = jnp.concatenate(
        [
            at_rank_t * (pair_doc.reshape(1, pairs) + 1).astype(f32),
            at_rank_t * (pair_slot.reshape(1, pairs) + 1).astype(f32),
        ],
        axis=0,
    ).astype(bf16)
    picked = lax.dot_general(
        hits_t, tagged_t, (((1,), (1,)), ((), ())), preferred_element_type=f32
    ).astype(jnp.int32)
    send_doc = picked[:, :capacity].reshape(devices * capacity) - 1
    slot_plus = picked[:, capacity:].reshape(devices * capacity)
    first_doc, second_doc = send_doc[: group * capacity], send_doc[group * capacity :]

    lanes = 128
    wide = width + lanes
    doc_part = (first_doc[:, None] == jnp.arange(docs, dtype=jnp.int32)[None, :]).astype(bf16)
    table = jnp.concatenate([doc_embed, jnp.zeros((docs, lanes), bf16)], axis=1)
    lane = jnp.arange(wide, dtype=jnp.int32)[None, :]
    slot_pair = slot_plus.astype(f32).reshape(2, group * capacity)
    slot_lanes = jnp.where(
        lane == width, slot_pair[0][:, None], jnp.where(lane == width + 1, slot_pair[1][:, None], 0.0)
    )
    send_first = (jnp.dot(doc_part, table, preferred_element_type=f32) + slot_lanes).astype(bf16)
    pick = (second_doc[:, None] == jnp.arange(docs, dtype=jnp.int32)[None, :]).astype(bf16)
    send_second = jnp.dot(pick, doc_embed, preferred_element_type=f32).astype(bf16)

    got_first = lax.all_to_all(
        send_first.reshape(group, capacity, wide), near, split_axis=0, concat_axis=0, tiled=True
    ).reshape(group * capacity, wide)
    got_second = lax.all_to_all(
        send_second.reshape(group, capacity, width), near, split_axis=0, concat_axis=0, tiled=True
    ).reshape(group * capacity, width)
    first_slot = got_first[:, width].astype(jnp.int32) - 1
    second_slot = got_first[:, width + 1].astype(jnp.int32) - 1

    label_ids = jnp.arange(owned, dtype=jnp.int32)
    first_hot = (label_ids[:, None] == first_slot[None, :]).astype(bf16)
    mirror_part = jnp.dot(first_hot, got_first, preferred_element_type=f32)[:, :width]
    mirrored = lax.ppermute(mirror_part, "zh", [(0, 1), (1, 0)])
    second_hot = (label_ids[:, None] == second_slot[None, :]).astype(bf16)
    own_part = jnp.dot(second_hot, got_second, preferred_element_type=f32)
    label_sums = own_part + mirrored
    label_vectors = rms_scale(label_sums).astype(bf16)
    members = (jnp.arange(CLUSTERS, dtype=jnp.int32)[:, None] == label_cluster[None, :]).astype(bf16)
    partial_sums = jnp.dot(members, label_vectors, preferred_element_type=f32)

    if CLUSTERS % group == 0:
        share = CLUSTERS // group
        spread_c = ("y", "zl", "x", "core")
        parts = lax.all_to_all(
            partial_sums.reshape(group, share, width), spread_c, split_axis=0, concat_axis=0, tiled=True
        )
        half_sums = jnp.sum(parts, axis=0)
        sums = half_sums + lax.ppermute(half_sums, "zh", [(0, 1), (1, 0)])
        own = rms_scale(sums).astype(bf16)
        centroids = lax.all_to_all(
            jnp.broadcast_to(own[None], (group, share, width)),
            spread_c,
            split_axis=0,
            concat_axis=0,
            tiled=True,
        ).reshape(CLUSTERS, width)
    else:
        centroids = rms_scale(lax.psum(partial_sums, axes)).astype(bf16)
    inner = lax.dot_general(
        label_vectors, centroids, (((1,), (1,)), ((), ())), preferred_element_type=f32
    )
    distances = 1.0 - inner / float(width)
    return (label_vectors, centroids, distances)


def solution(mesh):
    rows, cols = mesh.shape["row"], mesh.shape["col"]
    spread = ("y", "core", "zh", "zl", "x")
    split = Mesh(mesh.devices.reshape(rows // 2, 2, 2, 2, cols // 4), spread)
    placed = (P(spread, None), P(spread), P(spread, None), P(spread), P(spread))
    return jax.shard_map(
        local,
        mesh=split,
        in_specs=placed,
        out_specs=(P(spread, None), P(), P(spread, None)),
        check_vma=False,
    )
```

```python
import jax
import jax.numpy as jnp
from jax import lax
from jax.sharding import Mesh, PartitionSpec as P

CLUSTERS = 256


def rms_scale(values):
    return values * lax.rsqrt(jnp.mean(values * values, axis=-1, keepdims=True) + 1e-06)


def local(doc_embed, pair_doc, pair_owner, pair_slot, label_cluster):
    axes = ("y", "core", "zh", "zl", "x")
    near = ("y", "core", "x", "zl")
    devices = lax.axis_size(axes)
    halves = lax.axis_size(("zl", "x"))
    group = devices // 2
    pairs = pair_doc.shape[0]
    docs, width = doc_embed.shape
    owned = label_cluster.shape[0]
    capacity = 2 * pairs // devices
    f32, bf16 = jnp.float32, jnp.bfloat16

    me = lax.axis_index("zh")
    b = jnp.arange(devices, dtype=jnp.int32)
    b_later, b_proxy = b // group, b % group
    b_zh = jnp.where(b_later == 1, me, 1 - me)
    place = {}
    for name in reversed(near):
        size = lax.axis_size(name)
        place[name], b_proxy = b_proxy % size, b_proxy // size
    b_row = place["y"] * 2 + place["core"]
    b_zr = place["zl"] * lax.axis_size("x") + place["x"]
    block_owner = b_row * (2 * halves) + b_zh * halves + b_zr

    owner_row = pair_owner.reshape(1, pairs)
    hits_t = (block_owner[:, None] == owner_row).astype(bf16)
    pid = jnp.arange(pairs, dtype=jnp.int32)
    earlier_t = (pid[:, None] < pid[None, :]).astype(bf16)
    before_t = jnp.dot(hits_t, earlier_t, preferred_element_type=f32)
    rank_row = jnp.sum(before_t * hits_t.astype(f32), axis=0, keepdims=True).astype(jnp.int32)

    at_rank_t = (jnp.arange(capacity, dtype=jnp.int32)[:, None] == rank_row).astype(f32)
    tagged_t = jnp.concatenate(
        [
            at_rank_t * (pair_doc.reshape(1, pairs) + 1).astype(f32),
            at_rank_t * (pair_slot.reshape(1, pairs) + 1).astype(f32),
        ],
        axis=0,
    ).astype(bf16)
    picked = lax.dot_general(
        hits_t, tagged_t, (((1,), (1,)), ((), ())), preferred_element_type=f32
    ).astype(jnp.int32)
    send_doc = picked[:, :capacity].reshape(devices * capacity) - 1
    slot_plus = picked[:, capacity:].reshape(devices * capacity)
    first_doc, second_doc = send_doc[: group * capacity], send_doc[group * capacity :]

    lanes = 128
    wide = width + lanes
    doc_part = (first_doc[:, None] == jnp.arange(docs, dtype=jnp.int32)[None, :]).astype(bf16)
    table = jnp.concatenate([doc_embed, jnp.zeros((docs, lanes), bf16)], axis=1)
    lane = jnp.arange(wide, dtype=jnp.int32)[None, :]
    slot_pair = slot_plus.astype(bf16).reshape(2, group * capacity)
    zero = jnp.zeros((), bf16)
    slot_lanes = jnp.where(
        lane == width, slot_pair[0][:, None], jnp.where(lane == width + 1, slot_pair[1][:, None], zero)
    )
    send_first = jnp.dot(doc_part, table, preferred_element_type=bf16) + slot_lanes
    pick = (second_doc[:, None] == jnp.arange(docs, dtype=jnp.int32)[None, :]).astype(bf16)
    send_second = jnp.dot(pick, doc_embed, preferred_element_type=bf16)

    got_first = lax.all_to_all(
        send_first.reshape(group, capacity, wide), near, split_axis=0, concat_axis=0, tiled=True
    ).reshape(group * capacity, wide)
    got_second = lax.all_to_all(
        send_second.reshape(group, capacity, width), near, split_axis=0, concat_axis=0, tiled=True
    ).reshape(group * capacity, width)
    first_slot = got_first[:, width].astype(jnp.int32) - 1
    second_slot = got_first[:, width + 1].astype(jnp.int32) - 1

    label_ids = jnp.arange(owned, dtype=jnp.int32)
    first_hot = (label_ids[:, None] == first_slot[None, :]).astype(bf16)
    mirror_part = jnp.dot(first_hot, got_first, preferred_element_type=f32)[:, :width]
    mirrored = lax.ppermute(mirror_part, "zh", [(0, 1), (1, 0)])
    second_hot = (label_ids[:, None] == second_slot[None, :]).astype(bf16)
    own_part = jnp.dot(second_hot, got_second, preferred_element_type=f32)
    label_sums = own_part + mirrored
    label_vectors = rms_scale(label_sums).astype(bf16)
    members = (jnp.arange(CLUSTERS, dtype=jnp.int32)[:, None] == label_cluster[None, :]).astype(bf16)
    partial_sums = jnp.dot(members, label_vectors, preferred_element_type=f32)

    if CLUSTERS % group == 0:
        share = CLUSTERS // group
        parts = lax.all_to_all(
            partial_sums.reshape(group, share, width), near, split_axis=0, concat_axis=0, tiled=True
        )
        half_sums = jnp.sum(parts, axis=0)
        sums = half_sums + lax.ppermute(half_sums, "zh", [(0, 1), (1, 0)])
        own = rms_scale(sums).astype(bf16)
        centroids = lax.all_to_all(
            jnp.broadcast_to(own[None], (group, share, width)),
            near,
            split_axis=0,
            concat_axis=0,
            tiled=True,
        ).reshape(CLUSTERS, width)
    else:
        centroids = rms_scale(lax.psum(partial_sums, axes)).astype(bf16)
    inner = lax.dot_general(
        label_vectors, centroids, (((1,), (1,)), ((), ())), preferred_element_type=f32
    )
    distances = 1.0 - inner / float(width)
    return (label_vectors, centroids, distances)


def solution(mesh):
    rows, cols = mesh.shape["row"], mesh.shape["col"]
    spread = ("y", "core", "zh", "zl", "x")
    split = Mesh(mesh.devices.reshape(rows // 2, 2, 2, 2, cols // 4), spread)
    placed = (P(spread, None), P(spread), P(spread, None), P(spread), P(spread))
    return jax.shard_map(
        local,
        mesh=split,
        in_specs=placed,
        out_specs=(P(spread, None), P(), P(spread, None)),
        check_vma=False,
    )
```

```python
import jax
import jax.numpy as jnp
from jax import lax
from jax.sharding import Mesh, PartitionSpec as P

CLUSTERS = 256


def rms_scale(values):
    return values * lax.rsqrt(jnp.mean(values * values, axis=-1, keepdims=True) + 1e-06)


def local(doc_embed, pair_doc, pair_owner, pair_slot, label_cluster):
    axes = ("y", "core", "zh", "zl", "x")
    near = ("y", "core", "x", "zl")
    devices = lax.axis_size(axes)
    halves = lax.axis_size(("zl", "x"))
    group = devices // 2
    pairs = pair_doc.shape[0]
    docs, width = doc_embed.shape
    owned = label_cluster.shape[0]
    capacity = 2 * pairs // devices
    f32, bf16 = jnp.float32, jnp.bfloat16

    me = lax.axis_index("zh")
    b = jnp.arange(devices, dtype=jnp.int32)
    b_later, b_proxy = b // group, b % group
    b_zh = jnp.where(b_later == 1, me, 1 - me)
    place = {}
    for name in reversed(near):
        size = lax.axis_size(name)
        place[name], b_proxy = b_proxy % size, b_proxy // size
    b_row = place["y"] * 2 + place["core"]
    b_zr = place["zl"] * lax.axis_size("x") + place["x"]
    block_owner = b_row * (2 * halves) + b_zh * halves + b_zr

    owner_row = pair_owner.reshape(1, pairs)
    hits_t = (block_owner[:, None] == owner_row).astype(bf16)
    pid = jnp.arange(pairs, dtype=jnp.int32)
    earlier_t = (pid[:, None] < pid[None, :]).astype(bf16)
    before_t = jnp.dot(hits_t, earlier_t, preferred_element_type=f32)
    rank_row = jnp.sum(before_t * hits_t.astype(f32), axis=0, keepdims=True).astype(jnp.int32)

    at_rank_t = (jnp.arange(capacity, dtype=jnp.int32)[:, None] == rank_row).astype(bf16)
    hits_f = hits_t.astype(f32)
    tagged_t = jnp.concatenate(
        [
            hits_f * (pair_doc.reshape(1, pairs) + 1).astype(f32),
            hits_f * (pair_slot.reshape(1, pairs) + 1).astype(f32),
        ],
        axis=0,
    ).astype(bf16)
    picked = lax.dot_general(
        tagged_t, at_rank_t, (((1,), (1,)), ((), ())), preferred_element_type=f32
    ).astype(jnp.int32)
    send_doc = picked[:devices].reshape(devices * capacity) - 1
    slot_plus = picked[devices:].reshape(devices * capacity)
    first_doc, second_doc = send_doc[: group * capacity], send_doc[group * capacity :]

    lanes = 128
    wide = width + lanes
    doc_part = (first_doc[:, None] == jnp.arange(docs, dtype=jnp.int32)[None, :]).astype(bf16)
    table = jnp.concatenate([doc_embed, jnp.zeros((docs, lanes), bf16)], axis=1)
    lane = jnp.arange(wide, dtype=jnp.int32)[None, :]
    slot_pair = slot_plus.astype(bf16).reshape(2, group * capacity)
    zero = jnp.zeros((), bf16)
    slot_lanes = jnp.where(
        lane == width, slot_pair[0][:, None], jnp.where(lane == width + 1, slot_pair[1][:, None], zero)
    )
    send_first = jnp.dot(doc_part, table, preferred_element_type=bf16) + slot_lanes
    pick = (second_doc[:, None] == jnp.arange(docs, dtype=jnp.int32)[None, :]).astype(bf16)
    send_second = jnp.dot(pick, doc_embed, preferred_element_type=bf16)

    got_first = lax.all_to_all(
        send_first.reshape(group, capacity, wide), near, split_axis=0, concat_axis=0, tiled=True
    ).reshape(group * capacity, wide)
    got_second = lax.all_to_all(
        send_second.reshape(group, capacity, width), near, split_axis=0, concat_axis=0, tiled=True
    ).reshape(group * capacity, width)
    first_slot = got_first[:, width].astype(jnp.int32) - 1
    second_slot = got_first[:, width + 1].astype(jnp.int32) - 1

    label_ids = jnp.arange(owned, dtype=jnp.int32)
    first_hot = (label_ids[:, None] == first_slot[None, :]).astype(bf16)
    mirror_part = jnp.dot(first_hot, got_first[:, :width], preferred_element_type=f32)
    mirrored = lax.ppermute(mirror_part, "zh", [(0, 1), (1, 0)])
    second_hot = (label_ids[:, None] == second_slot[None, :]).astype(bf16)
    own_part = jnp.dot(second_hot, got_second, preferred_element_type=f32)
    label_sums = own_part + mirrored
    label_vectors = rms_scale(label_sums).astype(bf16)
    members = (jnp.arange(CLUSTERS, dtype=jnp.int32)[:, None] == label_cluster[None, :]).astype(bf16)
    partial_sums = jnp.dot(members, label_vectors, preferred_element_type=f32)

    if CLUSTERS % group == 0:
        share = CLUSTERS // group
        parts = lax.all_to_all(
            partial_sums.reshape(group, share, width), near, split_axis=0, concat_axis=0, tiled=True
        )
        half_sums = jnp.sum(parts, axis=0)
        sums = half_sums + lax.ppermute(half_sums, "zh", [(0, 1), (1, 0)])
        own = rms_scale(sums).astype(bf16)
        centroids = lax.all_to_all(
            jnp.broadcast_to(own[None], (group, share, width)),
            near,
            split_axis=0,
            concat_axis=0,
            tiled=True,
        ).reshape(CLUSTERS, width)
    else:
        centroids = rms_scale(lax.psum(partial_sums, axes)).astype(bf16)
    inner = lax.dot_general(
        label_vectors, centroids, (((1,), (1,)), ((), ())), preferred_element_type=f32
    )
    distances = 1.0 - inner / float(width)
    return (label_vectors, centroids, distances)


def solution(mesh):
    rows, cols = mesh.shape["row"], mesh.shape["col"]
    spread = ("y", "core", "zh", "zl", "x")
    split = Mesh(mesh.devices.reshape(rows // 2, 2, 2, 2, cols // 4), spread)
    placed = (P(spread, None), P(spread), P(spread, None), P(spread), P(spread))
    return jax.shard_map(
        local,
        mesh=split,
        in_specs=placed,
        out_specs=(P(spread, None), P(), P(spread, None)),
        check_vma=False,
    )
```

```python
import jax
import jax.numpy as jnp
from jax import lax
from jax.sharding import Mesh, PartitionSpec as P

CLUSTERS = 256


def rms_scale(values):
    return values * lax.rsqrt(jnp.mean(values * values, axis=-1, keepdims=True) + 1e-06)


def local(doc_embed, pair_doc, pair_owner, pair_slot, label_cluster):
    axes = ("y", "core", "zh", "zl", "x")
    near = ("y", "core", "x", "zl")
    devices = lax.axis_size(axes)
    halves = lax.axis_size(("zl", "x"))
    group = devices // 2
    pairs = pair_doc.shape[0]
    docs, width = doc_embed.shape
    owned = label_cluster.shape[0]
    capacity = 2 * pairs // devices
    f32, bf16 = jnp.float32, jnp.bfloat16

    me = lax.axis_index("zh")
    b = jnp.arange(devices, dtype=jnp.int32)
    b_later, b_proxy = b // group, b % group
    b_zh = jnp.where(b_later == 1, me, 1 - me)
    place = {}
    for name in reversed(near):
        size = lax.axis_size(name)
        place[name], b_proxy = b_proxy % size, b_proxy // size
    b_row = place["y"] * 2 + place["core"]
    b_zr = place["zl"] * lax.axis_size("x") + place["x"]
    block_owner = b_row * (2 * halves) + b_zh * halves + b_zr

    owner_row = pair_owner.reshape(1, pairs)
    hits_t = (block_owner[:, None] == owner_row).astype(bf16)
    pid = jnp.arange(pairs, dtype=jnp.int32)
    earlier_t = (pid[:, None] < pid[None, :]).astype(bf16)
    before_t = jnp.dot(hits_t, earlier_t, preferred_element_type=f32)
    rank_row = jnp.sum(before_t * hits_t.astype(f32), axis=0, keepdims=True).astype(jnp.int32)

    at_rank_t = (jnp.arange(capacity, dtype=jnp.int32)[:, None] == rank_row).astype(f32)
    tagged_t = jnp.concatenate(
        [
            at_rank_t * (pair_doc.reshape(1, pairs) + 1).astype(f32),
            at_rank_t * (pair_slot.reshape(1, pairs) + 1).astype(f32),
        ],
        axis=0,
    ).astype(bf16)
    picked = lax.dot_general(
        hits_t, tagged_t, (((1,), (1,)), ((), ())), preferred_element_type=f32
    ).astype(jnp.int32)
    send_doc = picked[:, :capacity].reshape(devices * capacity) - 1
    slot_plus = picked[:, capacity:].reshape(devices * capacity)
    first_doc, second_doc = send_doc[: group * capacity], send_doc[group * capacity :]

    lanes = 128
    wide = width + lanes
    doc_part = (first_doc[:, None] == jnp.arange(docs, dtype=jnp.int32)[None, :]).astype(bf16)
    slot_part = slot_plus.astype(bf16).reshape(2, group * capacity).T
    chooser = jnp.concatenate([doc_part, slot_part], axis=1)
    table = jnp.concatenate(
        [
            jnp.concatenate([doc_embed, jnp.zeros((docs, lanes), bf16)], axis=1),
            jnp.concatenate([jnp.zeros((2, width), bf16), jnp.eye(2, lanes, dtype=bf16)], axis=1),
        ],
        axis=0,
    )
    send_first = jnp.dot(chooser, table, preferred_element_type=bf16)
    pick = (second_doc[:, None] == jnp.arange(docs, dtype=jnp.int32)[None, :]).astype(bf16)
    send_second = jnp.dot(pick, doc_embed, preferred_element_type=f32).astype(bf16)

    got_first = lax.all_to_all(
        send_first.reshape(group, capacity, wide), near, split_axis=0, concat_axis=0, tiled=True
    ).reshape(group * capacity, wide)
    got_second = lax.all_to_all(
        send_second.reshape(group, capacity, width), near, split_axis=0, concat_axis=0, tiled=True
    ).reshape(group * capacity, width)
    first_slot = got_first[:, width].astype(jnp.int32) - 1
    second_slot = got_first[:, width + 1].astype(jnp.int32) - 1

    label_ids = jnp.arange(owned, dtype=jnp.int32)
    first_hot = (label_ids[:, None] == first_slot[None, :]).astype(bf16)
    mirror_part = jnp.dot(first_hot, got_first, preferred_element_type=f32)[:, :width]
    mirrored = lax.ppermute(mirror_part, "zh", [(0, 1), (1, 0)])
    second_hot = (label_ids[:, None] == second_slot[None, :]).astype(bf16)
    own_part = jnp.dot(second_hot, got_second, preferred_element_type=f32)
    label_sums = own_part + mirrored
    label_vectors = rms_scale(label_sums).astype(bf16)
    members = (jnp.arange(CLUSTERS, dtype=jnp.int32)[:, None] == label_cluster[None, :]).astype(bf16)
    partial_sums = jnp.dot(members, label_vectors, preferred_element_type=f32)

    if CLUSTERS % group == 0:
        share = CLUSTERS // group
        parts = lax.all_to_all(
            partial_sums.reshape(group, share, width), near, split_axis=0, concat_axis=0, tiled=True
        )
        half_sums = jnp.sum(parts, axis=0)
        sums = half_sums + lax.ppermute(half_sums, "zh", [(0, 1), (1, 0)])
        own = rms_scale(sums).astype(bf16)
        centroids = lax.all_to_all(
            jnp.broadcast_to(own[None], (group, share, width)),
            near,
            split_axis=0,
            concat_axis=0,
            tiled=True,
        ).reshape(CLUSTERS, width)
    else:
        centroids = rms_scale(lax.psum(partial_sums, axes)).astype(bf16)
    inner = lax.dot_general(
        label_vectors, centroids, (((1,), (1,)), ((), ())), preferred_element_type=f32
    )
    distances = 1.0 - inner / float(width)
    return (label_vectors, centroids, distances)


def solution(mesh):
    rows, cols = mesh.shape["row"], mesh.shape["col"]
    spread = ("y", "core", "zh", "zl", "x")
    split = Mesh(mesh.devices.reshape(rows // 2, 2, 2, 2, cols // 4), spread)
    placed = (P(spread, None), P(spread), P(spread, None), P(spread), P(spread))
    return jax.shard_map(
        local,
        mesh=split,
        in_specs=placed,
        out_specs=(P(spread, None), P(), P(spread, None)),
        check_vma=False,
    )
```

```python
import jax
import jax.numpy as jnp
from jax import lax
from jax.sharding import Mesh, PartitionSpec as P

CLUSTERS = 256


def rms_scale(values):
    return values * lax.rsqrt(jnp.mean(values * values, axis=-1, keepdims=True) + 1e-06)


def local(doc_embed, pair_doc, pair_owner, pair_slot, label_cluster):
    axes = ("y", "core", "zh", "zl", "x")
    near = ("y", "core", "x", "zl")
    devices = lax.axis_size(axes)
    halves = lax.axis_size(("zl", "x"))
    group = devices // 2
    pairs = pair_doc.shape[0]
    docs, width = doc_embed.shape
    owned = label_cluster.shape[0]
    capacity = 2 * pairs // devices
    f32, bf16 = jnp.float32, jnp.bfloat16

    me = lax.axis_index("zh")
    b = jnp.arange(devices, dtype=jnp.int32)
    b_later, b_proxy = b // group, b % group
    b_zh = jnp.where(b_later == 1, me, 1 - me)
    place = {}
    for name in reversed(near):
        size = lax.axis_size(name)
        place[name], b_proxy = b_proxy % size, b_proxy // size
    b_row = place["y"] * 2 + place["core"]
    b_zr = place["zl"] * lax.axis_size("x") + place["x"]
    block_owner = b_row * (2 * halves) + b_zh * halves + b_zr

    owner_row = pair_owner.reshape(1, pairs)
    hits_t = (block_owner[:, None] == owner_row).astype(bf16)
    pid = jnp.arange(pairs, dtype=jnp.int32)
    earlier_t = (pid[:, None] < pid[None, :]).astype(bf16)
    before_t = jnp.dot(hits_t, earlier_t, preferred_element_type=f32)
    rank_row = jnp.sum(before_t * hits_t.astype(f32), axis=0, keepdims=True).astype(jnp.int32)

    at_rank_t = (jnp.arange(capacity, dtype=jnp.int32)[:, None] == rank_row).astype(f32)
    tagged_t = jnp.concatenate(
        [
            at_rank_t * (pair_doc.reshape(1, pairs) + 1).astype(f32),
            at_rank_t * (pair_slot.reshape(1, pairs) + 1).astype(f32),
        ],
        axis=0,
    ).astype(bf16)
    picked = lax.dot_general(
        hits_t, tagged_t, (((1,), (1,)), ((), ())), preferred_element_type=f32
    ).astype(jnp.int32)
    send_doc = picked[:, :capacity].reshape(devices * capacity) - 1
    slot_plus = picked[:, capacity:].reshape(devices * capacity)
    first_doc, second_doc = send_doc[: group * capacity], send_doc[group * capacity :]

    lanes = 128
    wide = width + lanes
    doc_part = (first_doc[:, None] == jnp.arange(docs, dtype=jnp.int32)[None, :]).astype(bf16)
    table = jnp.concatenate([doc_embed, jnp.zeros((docs, lanes), bf16)], axis=1)
    lane = jnp.arange(wide, dtype=jnp.int32)[None, :]
    slot_pair = slot_plus.astype(f32).reshape(2, group * capacity)
    slot_lanes = jnp.where(
        lane == width, slot_pair[0][:, None], jnp.where(lane == width + 1, slot_pair[1][:, None], 0.0)
    )
    send_first = (jnp.dot(doc_part, table, preferred_element_type=f32) + slot_lanes).astype(bf16)
    pick = (second_doc[:, None] == jnp.arange(docs, dtype=jnp.int32)[None, :]).astype(bf16)
    send_second = jnp.dot(pick, doc_embed, preferred_element_type=f32).astype(bf16)

    got_first = lax.all_to_all(
        send_first.reshape(group, capacity, wide), near, split_axis=0, concat_axis=0, tiled=True
    ).reshape(group * capacity, wide)
    first_slot = got_first[:, width].astype(jnp.int32) - 1
    second_slot = got_first[:, width + 1].astype(jnp.int32) - 1

    label_ids = jnp.arange(owned, dtype=jnp.int32)
    first_hot = (label_ids[:, None] == first_slot[None, :]).astype(bf16)
    mirror_part = jnp.dot(first_hot, got_first, preferred_element_type=f32)[:, :width]
    send_second, mirror_part = lax.optimization_barrier((send_second, mirror_part))
    mirrored = lax.ppermute(mirror_part, "zh", [(0, 1), (1, 0)])
    got_second = lax.all_to_all(
        send_second.reshape(group, capacity, width), near, split_axis=0, concat_axis=0, tiled=True
    ).reshape(group * capacity, width)
    second_hot = (label_ids[:, None] == second_slot[None, :]).astype(bf16)
    own_part = jnp.dot(second_hot, got_second, preferred_element_type=f32)
    label_sums = own_part + mirrored
    label_vectors = rms_scale(label_sums).astype(bf16)
    members = (jnp.arange(CLUSTERS, dtype=jnp.int32)[:, None] == label_cluster[None, :]).astype(bf16)
    partial_sums = jnp.dot(members, label_vectors, preferred_element_type=f32)

    if CLUSTERS % group == 0:
        share = CLUSTERS // group
        parts = lax.all_to_all(
            partial_sums.reshape(group, share, width), near, split_axis=0, concat_axis=0, tiled=True
        )
        half_sums = jnp.sum(parts, axis=0)
        sums = half_sums + lax.ppermute(half_sums, "zh", [(0, 1), (1, 0)])
        own = rms_scale(sums).astype(bf16)
        centroids = lax.all_to_all(
            jnp.broadcast_to(own[None], (group, share, width)),
            near,
            split_axis=0,
            concat_axis=0,
            tiled=True,
        ).reshape(CLUSTERS, width)
    else:
        centroids = rms_scale(lax.psum(partial_sums, axes)).astype(bf16)
    inner = lax.dot_general(
        label_vectors, centroids, (((1,), (1,)), ((), ())), preferred_element_type=f32
    )
    distances = 1.0 - inner / float(width)
    return (label_vectors, centroids, distances)


def solution(mesh):
    rows, cols = mesh.shape["row"], mesh.shape["col"]
    spread = ("y", "core", "zh", "zl", "x")
    split = Mesh(mesh.devices.reshape(rows // 2, 2, 2, 2, cols // 4), spread)
    placed = (P(spread, None), P(spread), P(spread, None), P(spread), P(spread))
    return jax.shard_map(
        local,
        mesh=split,
        in_specs=placed,
        out_specs=(P(spread, None), P(), P(spread, None)),
        check_vma=False,
    )
```
